512 devices in a mesh: dp: 16 (over z_lo, core), ctx: 32 (over y, x, z_hi).
Axes of the slice: x: 4, y: 4, z: 16 (z_hi: 2, z_lo: 8; z = z_hi * 8 + z_lo), core: 2. Of those that a mesh axis runs over, the one named last changes fastest.
Arguments:
- queries: bfloat16 [131072, 256], P(('dp', 'ctx')), parts along dimension 0, may hold values from -6 to 6
- keys: bfloat16 [131072, 256], P(('dp', 'ctx')), parts along dimension 0, may hold values from -6 to 6
- values: bfloat16 [131072, 256], P(('dp', 'ctx')), parts along dimension 0, may hold values from -6 to 6
- out_grad: bfloat16 [131072, 256], P(('dp', 'ctx')), parts along dimension 0, may hold values from -16 to 16
- block_list: int32 [1024, 7], P(('dp', 'ctx')), parts along dimension 0, may hold values from -1 to 63, as said below
- causal: int32 [1024], P(('dp', 'ctx')), parts along dimension 0, may hold values 0 or 1
Outputs:
- query_grad: bfloat16 [131072, 256], P(('dp', 'ctx')), parts along dimension 0
- key_grad: bfloat16 [131072, 256], P(('dp', 'ctx')), parts along dimension 0
- value_grad: bfloat16 [131072, 256], P(('dp', 'ctx')), parts along dimension 0
The draws below stay inside these ranges and needn't reach their ends.
There are 16 independent parts, one for each index of `dp`. The reference program is written for one: setup_inputs(seed, part) draws one part's arguments, and reference() takes and returns one part's arrays. A program takes and returns all parts, laid end to end along the dimension named above; each array names one. Nothing has to cross between parts.
Inputs may be any that keep to these rules, and one draw needn't show every extreme that they name: `block_list`: entry 0 of block b is b; entry j, for j from 1 to 6, is b - 2**(j-1) or -1, and is -1 where that would be negative.
All inputs are finite; a program needn't handle non-finite values. No bound on the sum of `causal` on one device may be relied on, other than what follows from the above.
Results may differ from the reference program's by a relative error of at most 0.034.
Values may be sent and summed in bfloat16 or wider, within the bound.
No kernel may reach another device: no remote copies, remote signals or barrier semaphores. Data moves between devices by JAX's collectives and lax.ppermute only.
A program may use at most 64 MiB of HBM per device.

```python
import jax
import jax.numpy as jnp
from jax import lax

BLOCK = 128
HEADS = 2
HEAD_DIM = 128
SEQ = 8192
BPD = 2
NB = 64
LEVELS = 6
ENTRIES = 7


def drawn_pair(key):
    feat = HEADS * HEAD_DIM
    base_q = jnp.clip(jax.random.normal(jax.random.fold_in(key, 11), (SEQ, feat), jnp.float32), -6.0, 6.0)
    base_k = jnp.clip(jax.random.normal(jax.random.fold_in(key, 12), (SEQ, feat), jnp.float32), -6.0, 6.0)
    return (base_q, base_k)


def draw_queries(key, part):
    return drawn_pair(key)[0].astype(jnp.bfloat16)


def draw_keys(key, part):
    return drawn_pair(key)[1].astype(jnp.bfloat16)


def draw_block_list(key, part):
    block_ids = jnp.arange(NB, dtype=jnp.int32)
    reaches = jnp.left_shift(jnp.int32(1), jnp.arange(LEVELS, dtype=jnp.int32))
    target = block_ids[:, None] - reaches[None, :]
    keeper = jax.random.randint(jax.random.fold_in(key, 21), (NB, LEVELS), 0, 4) > 0
    listed = jnp.where((target >= 0) & keeper, target, -1).astype(jnp.int32)
    return jnp.concatenate([block_ids[:, None], listed], 1)


def place_ends(entries, stream_key, smallest, high):
    spot = [jax.random.randint(jax.random.fold_in(stream_key, axis), (), 0, length) for axis, length in enumerate(entries.shape)]
    longest = entries.shape.index(max(entries.shape))
    beside = spot[:longest] + [(spot[longest] + 1) % entries.shape[longest]] + spot[longest + 1:]
    return entries.at[tuple(spot)].set(smallest).at[tuple(beside)].set(high)


def levels(rng, extent, pieces, smallest, top_value):
    loudness = 1.0
    for dim, parts in pieces:
        heights = jax.random.uniform(jax.random.fold_in(jax.random.fold_in(rng, 6), dim), (parts,), jnp.float32, smallest / len(pieces), top_value / len(pieces))
        loudness = loudness * jnp.repeat(jnp.exp(heights), extent[dim] // parts).reshape((-1,) + (1,) * (len(extent) - 1 - dim))
    return loudness


def centred(stream_key, dims, scale, bound, pieces=(), held_as=jnp.bfloat16):
    entries = scale * jax.random.normal(stream_key, dims, jnp.float32)
    if pieces:
        entries = entries * levels(stream_key, dims, pieces, -0.22, 0.18)
    return jnp.clip(entries, -bound, bound).astype(held_as)


def setup_inputs(seed: int = 0, part: int = 0) -> dict:
    seeds = jax.random.split(jax.random.key(seed), 7)
    part_keys = jax.random.split(jax.random.fold_in(seeds[6], part), 7)
    queries = draw_queries(jax.random.fold_in(jax.random.fold_in(seeds[6], part), 71), part)
    keys = draw_keys(jax.random.fold_in(jax.random.fold_in(seeds[6], part), 71), part)
    values = centred(part_keys[2], (SEQ, HEADS * HEAD_DIM), 1.0, 6.0, ((0, 32),))
    out_grad = centred(part_keys[3], (SEQ, HEADS * HEAD_DIM), 4.0, 16.0, ((0, 32),))
    block_list = draw_block_list(jax.random.fold_in(jax.random.fold_in(seeds[6], part), 71), part)
    causal = place_ends((jax.random.randint(part_keys[5], (NB,), 0, 4) < 3).astype(jnp.int32), jax.random.fold_in(part_keys[5], 1), 0, 1)
    return dict(queries=queries, keys=keys, values=values, out_grad=out_grad, block_list=block_list, causal=causal)


def reference(queries, keys, values, out_grad, block_list, causal):
    feat = HEADS * HEAD_DIM
    scale = HEAD_DIM ** -0.5
    q_blocks = queries.reshape(NB, BLOCK, HEADS, HEAD_DIM)
    k_blocks = keys.reshape(NB, BLOCK, HEADS, HEAD_DIM)
    v_blocks = values.reshape(NB, BLOCK, HEADS, HEAD_DIM)
    g_blocks = out_grad.reshape(NB, BLOCK, HEADS, HEAD_DIM)
    positions = jnp.arange(BLOCK)
    lower = positions[:, None] >= positions[None, :]
    level_ids = jnp.arange(ENTRIES)

    def one_block(index):
        entry_row = block_list[index]
        valid = entry_row >= 0
        safe = jnp.maximum(entry_row, 0).astype(jnp.int32)
        key_set = k_blocks[safe].astype(jnp.float32)
        value_set = v_blocks[safe].astype(jnp.float32)
        query_here = q_blocks[index].astype(jnp.float32)
        grad_here = g_blocks[index].astype(jnp.float32)
        scores = jnp.einsum('thd,euhd->hteu', query_here, key_set) * scale
        self_mask = jnp.where(causal[index] > 0, lower, True)
        mask = jnp.where(level_ids[None, :, None] == 0, self_mask[:, None, :], True)
        mask = mask & valid[None, :, None]
        scores = jnp.where(mask[None], scores, -jnp.inf)
        top = jnp.max(scores, axis=(2, 3))
        lse = top + jnp.log(jnp.sum(jnp.exp(scores - top[:, :, None, None]), axis=(2, 3)))
        probs = jnp.exp(scores - lse[:, :, None, None])
        weights = probs.astype(jnp.bfloat16).astype(jnp.float32)
        dprobs = jnp.einsum('thd,euhd->hteu', grad_here, value_set)
        delta = jnp.sum(weights * dprobs, axis=(2, 3))
        dscores = (probs * (dprobs - delta[:, :, None, None])).astype(jnp.bfloat16).astype(jnp.float32)
        query_part = (jnp.einsum('hteu,euhd->thd', dscores, key_set) * scale).astype(jnp.bfloat16)
        key_part = jnp.einsum('hteu,thd->euhd', dscores, query_here) * scale
        value_part = jnp.einsum('hteu,thd->euhd', weights, grad_here)
        return (query_part.reshape(BLOCK, feat), key_part.reshape(ENTRIES, BLOCK, feat),
                value_part.reshape(ENTRIES, BLOCK, feat))

    query_grad, key_terms, value_terms = lax.map(one_block, jnp.arange(NB))

    def collect(terms):
        local_sum = terms[:, 0]
        near_sum = jnp.zeros((NB, BLOCK, feat), jnp.float32)
        far_sums = []
        block_ids = jnp.arange(NB)
        for level in range(1, ENTRIES):
            reach = 2 ** (level - 1)
            moved = jnp.concatenate([terms[reach:, level], jnp.zeros((reach, BLOCK, feat), jnp.float32)], 0)
            if reach <= BPD:
                remote = ((block_ids + reach) // BPD != block_ids // BPD)[:, None, None]
                local_sum = local_sum + jnp.where(remote, 0.0, moved)
                near_sum = near_sum + jnp.where(remote, moved, 0.0)
            else:
                far_sums.append(lax.optimization_barrier(moved.astype(jnp.bfloat16)).astype(jnp.float32))
        total = local_sum + lax.optimization_barrier(near_sum.astype(jnp.bfloat16)).astype(jnp.float32)
        for piece in far_sums:
            total = total + piece
        return total.reshape(SEQ, feat).astype(jnp.bfloat16)

    return query_grad.reshape(SEQ, feat), collect(key_terms), collect(value_terms)
```

```python
import jax
import jax.numpy as jnp
from jax import lax
from jax.sharding import PartitionSpec as P

BLOCK = 128
HEADS = 2


def from_behind(value, axis, steps):
    count = lax.axis_size(axis)
    initial, last = (max(0, -steps), min(count, count - steps))
    return lax.ppermute(value, axis, [(source, source + steps) for source in range(initial, last)])


def on_device(queries, keys, values, out_grad, block_list, causal):
    tok_rows, feat = queries.shape
    blocks_here = tok_rows // BLOCK
    entries = block_list.shape[1]
    head_size = feat // HEADS
    scale = head_size ** (-0.5)
    far_levels = [level for level in range(1, entries) if 2 ** (level - 1) > blocks_here]
    near_levels = [level for level in range(1, entries) if 2 ** (level - 1) <= blocks_here]

    def to_blocks(array):
        return array.reshape(array.shape[:-2] + (blocks_here, BLOCK, HEADS, head_size))

    kv_own = jnp.concatenate([keys, values], 1)
    qg_own = jnp.concatenate([queries, out_grad], 1)
    kv_near = from_behind(kv_own, "ctx", 1)
    qg_next = from_behind(qg_own, "ctx", -1)
    kv_far = {}
    qg_far = {}
    for level in far_levels:
        distance = 2 ** (level - 1) // blocks_here
        kv_far[level] = from_behind(kv_own, "ctx", distance)
        qg_far[level] = from_behind(qg_own, "ctx", -distance)

    kv_joined = jnp.concatenate([kv_near, kv_own], 0)
    kv_levels = []
    for level in range(entries):
        if level == 0:
            kv_levels.append(kv_own)
        elif level in near_levels:
            start = (blocks_here - 2 ** (level - 1)) * BLOCK
            kv_levels.append(kv_joined[start : start + tok_rows])
        else:
            kv_levels.append(kv_far[level])
    kv_stack = jnp.stack(kv_levels, 0)
    k_stack = to_blocks(kv_stack[..., :feat])
    v_stack = to_blocks(kv_stack[..., feat:])
    q_blocks = to_blocks(queries)
    g_blocks = to_blocks(out_grad)

    positions = jnp.arange(BLOCK)
    lower = positions[:, None] >= positions[None, :]
    valid = block_list >= 0
    self_mask = jnp.where(causal[:, None, None] > 0, lower[None], True) & valid[:, 0, None, None]
    level_mask = jnp.concatenate(
        [self_mask[None], jnp.broadcast_to(valid.T[1:, :, None, None], (entries - 1, blocks_here, BLOCK, BLOCK))], 0
    )

    scores = jnp.einsum("bthd,lbuhd->lbhtu", q_blocks, k_stack, preferred_element_type=jnp.float32) * scale
    scores = jnp.where(level_mask[:, :, None], scores, -jnp.inf)
    top = scores.max(axis=(0, 4))
    lse = top + jnp.log(jnp.sum(jnp.exp(scores - top[None, ..., None]), axis=(0, 4)))
    probs = jnp.exp(scores - lse[None, ..., None])
    weights = probs.astype(jnp.bfloat16)
    dprobs = jnp.einsum("bthd,lbuhd->lbhtu", g_blocks, v_stack, preferred_element_type=jnp.float32)
    delta = jnp.sum(weights.astype(jnp.float32) * dprobs, axis=(0, 4))
    dscores = (probs * (dprobs - delta[None, ..., None])).astype(jnp.bfloat16)
    query_grad = jnp.einsum("lbhtu,lbuhd->bthd", dscores, k_stack, preferred_element_type=jnp.float32) * scale
    key_grad = jnp.einsum("bhtu,bthd->buhd", dscores[0], q_blocks, preferred_element_type=jnp.float32) * scale
    value_grad = jnp.einsum("bhtu,bthd->buhd", weights[0], g_blocks, preferred_element_type=jnp.float32)

    masked_lse = jnp.where(valid.T[:, :, None, None], lse[None], jnp.inf)
    stats_own = {level: jnp.stack([masked_lse[level], delta], 0) for level in range(1, entries)}
    near_stats = jnp.stack([stats_own[level] for level in near_levels], 0)
    near_back = from_behind(near_stats, "ctx", -1)
    stats_next = {level: near_back[index] for index, level in enumerate(near_levels)}
    far_back = {}
    for level in far_levels:
        distance = 2 ** (level - 1) // blocks_here
        far_back[level] = from_behind(stats_own[level], "ctx", -distance)

    qg_joined = jnp.concatenate([qg_own, qg_next], 0)
    qg_levels = []
    stat_levels = []
    for level in range(1, entries):
        reach = 2 ** (level - 1)
        if level in near_levels:
            start = reach * BLOCK
            qg_levels.append(qg_joined[start : start + tok_rows])
            joined_stats = jnp.concatenate([stats_own[level], stats_next[level]], 1)
            stat_levels.append(joined_stats[:, reach : reach + blocks_here])
        else:
            qg_levels.append(qg_far[level])
            stat_levels.append(far_back[level])
    qg_stack = jnp.stack(qg_levels, 0)
    stat_stack = jnp.stack(stat_levels, 0)
    qk_stack = to_blocks(qg_stack[..., :feat])
    gk_stack = to_blocks(qg_stack[..., feat:])
    k_blocks = to_blocks(keys)
    v_blocks = to_blocks(values)
    other_scores = jnp.einsum("lbthd,buhd->lbhtu", qk_stack, k_blocks, preferred_element_type=jnp.float32) * scale
    other_probs = jnp.exp(other_scores - stat_stack[:, 0, ..., None])
    other_weights = other_probs.astype(jnp.bfloat16)
    other_dprobs = jnp.einsum("lbthd,buhd->lbhtu", gk_stack, v_blocks, preferred_element_type=jnp.float32)
    other_dscores = (other_probs * (other_dprobs - stat_stack[:, 1, ..., None])).astype(jnp.bfloat16)
    key_grad = key_grad + jnp.einsum(
        "lbhtu,lbthd->buhd", other_dscores, qk_stack, preferred_element_type=jnp.float32
    ) * scale
    value_grad = value_grad + jnp.einsum(
        "lbhtu,lbthd->buhd", other_weights, gk_stack, preferred_element_type=jnp.float32
    )
    return (
        query_grad.astype(jnp.bfloat16).reshape(tok_rows, feat),
        key_grad.astype(jnp.bfloat16).reshape(tok_rows, feat),
        value_grad.astype(jnp.bfloat16).reshape(tok_rows, feat),
    )


def solution(mesh):
    return jax.shard_map(
        on_device,
        mesh=mesh,
        in_specs=(
            P(("dp", "ctx"), None),
            P(("dp", "ctx"), None),
            P(("dp", "ctx"), None),
            P(("dp", "ctx"), None),
            P(("dp", "ctx"), None),
            P(("dp", "ctx")),
        ),
        out_specs=(P(("dp", "ctx"), None), P(("dp", "ctx"), None), P(("dp", "ctx"), None)),
        check_vma=False,
    )
```

```python
import jax
import jax.numpy as jnp
from jax import lax
from jax.experimental import pallas as pl
from jax.experimental.pallas import tpu as pltpu
from jax.sharding import PartitionSpec as P

BLOCK = 128
HEADS = 2


def from_behind(value, axis, steps):
    count = lax.axis_size(axis)
    initial, last = (max(0, -steps), min(count, count - steps))
    return lax.ppermute(value, axis, [(source, source + steps) for source in range(initial, last)])


def dot_nt(a, b):
    return lax.dot_general(a, b, (((1,), (1,)), ((), ())), preferred_element_type=jnp.float32)


def dot_tn(a, b):
    return lax.dot_general(a, b, (((0,), (0,)), ((), ())), preferred_element_type=jnp.float32)


def dot_nn(a, b):
    return lax.dot_general(a, b, (((1,), (0,)), ((), ())), preferred_element_type=jnp.float32)


def lower_mask():
    rows = lax.broadcasted_iota(jnp.int32, (BLOCK, BLOCK), 0)
    cols = lax.broadcasted_iota(jnp.int32, (BLOCK, BLOCK), 1)
    return rows >= cols


def make_levels(blocks_here, entries):
    kinds = []
    for level in range(entries):
        reach = 2 ** (level - 1) if level > 0 else 0
        kinds.append((level, reach, "own" if level == 0 else ("near" if reach <= blocks_here else "far")))
    return kinds


def query_side(blocks_here, entries, head_size, scale):
    kinds = make_levels(blocks_here, entries)
    far_levels = [level for level, _, kind in kinds if kind == "far"]

    def kernel(list_ref, causal_ref, q_ref, g_ref, own_ref, near_ref, *rest):
        far_refs = dict(zip(far_levels, rest[: len(far_levels)]))
        dq_ref, stats_ref = rest[len(far_levels):]
        lower = lower_mask()
        for block in range(blocks_here):
            rows = slice(block * BLOCK, (block + 1) * BLOCK)
            valid = [list_ref[block, level] >= 0 for level in range(entries)]
            self_ok = jnp.logical_or(lower, causal_ref[block] == 0)
            for head in range(HEADS):
                kcols = slice(head * head_size, (head + 1) * head_size)
                vcols = slice((HEADS + head) * head_size, (HEADS + head + 1) * head_size)
                q = q_ref[rows, kcols]
                g = g_ref[rows, kcols]
                keys_at = []
                values_at = []
                for level, reach, kind in kinds:
                    if kind == "own":
                        src, at = own_ref, block
                    elif kind == "near":
                        joined = blocks_here + block - reach
                        src, at = (own_ref, joined - blocks_here) if joined >= blocks_here else (near_ref, joined)
                    else:
                        src, at = far_refs[level], block
                    keys_at.append(src[at * BLOCK : (at + 1) * BLOCK, kcols])
                    values_at.append(src[at * BLOCK : (at + 1) * BLOCK, vcols])
                scores = []
                for level in range(entries):
                    s = dot_nt(q, keys_at[level]) * scale
                    keep = jnp.logical_and(self_ok, valid[0]) if level == 0 else valid[level]
                    scores.append(jnp.where(keep, s, -jnp.inf))
                top = scores[0].max(axis=1, keepdims=True)
                for level in range(1, entries):
                    top = jnp.maximum(top, scores[level].max(axis=1, keepdims=True))
                total = jnp.zeros_like(top)
                for level in range(entries):
                    total = total + jnp.sum(jnp.exp(scores[level] - top), axis=1, keepdims=True)
                lse = top + jnp.log(total)
                probs = []
                dprobs = []
                delta = jnp.zeros_like(top)
                for level in range(entries):
                    p = jnp.exp(scores[level] - lse)
                    dp = dot_nt(g, values_at[level])
                    w = p.astype(jnp.bfloat16).astype(jnp.float32)
                    delta = delta + jnp.sum(w * dp, axis=1, keepdims=True)
                    probs.append(p)
                    dprobs.append(dp)
                dq = jnp.zeros((BLOCK, head_size), jnp.float32)
                for level in range(entries):
                    ds = (probs[level] * (dprobs[level] - delta)).astype(jnp.bfloat16)
                    dq = dq + dot_nn(ds, keys_at[level])
                dq_ref[rows, kcols] = (dq * scale).astype(dq_ref.dtype)
                stats_ref[rows, head : head + 1] = delta
                for level in range(entries):
                    col = HEADS + HEADS * level + head
                    stats_ref[rows, col : col + 1] = jnp.where(valid[level], lse, jnp.inf)

    return kernel, far_levels


def key_side(blocks_here, entries, head_size, scale):
    kinds = make_levels(blocks_here, entries)
    far_levels = [level for level, _, kind in kinds if kind == "far"]

    def kernel(list_ref, causal_ref, kv_ref, qg_ref, qg_next_ref, stats_ref, stats_next_ref, *rest):
        count = len(far_levels)
        far_qg = dict(zip(far_levels, rest[:count]))
        far_stats = dict(zip(far_levels, rest[count : 2 * count]))
        dk_ref, dv_ref = rest[2 * count :]
        lower = lower_mask()
        for block in range(blocks_here):
            rows = slice(block * BLOCK, (block + 1) * BLOCK)
            self_ok = jnp.logical_or(lower, causal_ref[block] == 0)
            for head in range(HEADS):
                kcols = slice(head * head_size, (head + 1) * head_size)
                vcols = slice((HEADS + head) * head_size, (HEADS + head + 1) * head_size)
                k = kv_ref[rows, kcols]
                v = kv_ref[rows, vcols]
                dk = jnp.zeros((BLOCK, head_size), jnp.float32)
                dv = jnp.zeros((BLOCK, head_size), jnp.float32)
                for level, reach, kind in kinds:
                    if kind == "own":
                        src, st, at = qg_ref, stats_ref, block
                    elif kind == "near":
                        joined = block + reach
                        if joined < blocks_here:
                            src, st, at = qg_ref, stats_ref, joined
                        else:
                            src, st, at = qg_next_ref, stats_next_ref, joined - blocks_here
                    else:
                        src, st, at = far_qg[level], far_stats[level], block
                    qrows = slice(at * BLOCK, (at + 1) * BLOCK)
                    q = src[qrows, kcols]
                    g = src[qrows, vcols]
                    col = HEADS + HEADS * level + head
                    lse = st[qrows, col : col + 1]
                    delta = st[qrows, head : head + 1]
                    s = dot_nt(q, k) * scale
                    if kind == "own":
                        s = jnp.where(self_ok, s, -jnp.inf)
                    p = jnp.exp(s - lse)
                    w = p.astype(jnp.bfloat16)
                    dp = dot_nt(g, v)
                    ds = (p * (dp - delta)).astype(jnp.bfloat16)
                    dk = dk + dot_tn(ds, q)
                    dv = dv + dot_tn(w, g)
                dk_ref[rows, kcols] = (dk * scale).astype(dk_ref.dtype)
                dv_ref[rows, kcols] = dv.astype(dv_ref.dtype)

    return kernel, far_levels


def vmem_specs(count):
    return [pl.BlockSpec(memory_space=pltpu.VMEM) for _ in range(count)]


def smem_specs(count):
    return [pl.BlockSpec(memory_space=pltpu.SMEM) for _ in range(count)]


def on_device(queries, keys, values, out_grad, block_list, causal):
    tok_rows, feat = queries.shape
    blocks_here = tok_rows // BLOCK
    entries = block_list.shape[1]
    head_size = feat // HEADS
    scale = head_size ** (-0.5)
    stat_cols = HEADS + HEADS * entries

    kv_own = jnp.concatenate([keys, values], 1)
    qg_own = jnp.concatenate([queries, out_grad], 1)
    kv_near = from_behind(kv_own, "ctx", 1)
    qg_next = from_behind(qg_own, "ctx", -1)
    q_kernel, far_levels = query_side(blocks_here, entries, head_size, scale)
    kv_far = []
    qg_far = []
    distances = [2 ** (level - 1) // blocks_here for level in far_levels]
    for distance in distances:
        kv_far.append(from_behind(kv_own, "ctx", distance))
        qg_far.append(from_behind(qg_own, "ctx", -distance))

    query_grad, stats = pl.pallas_call(
        q_kernel,
        out_shape=(
            jax.ShapeDtypeStruct((tok_rows, feat), jnp.bfloat16),
            jax.ShapeDtypeStruct((tok_rows, stat_cols), jnp.float32),
        ),
        in_specs=smem_specs(2) + vmem_specs(4 + len(kv_far)),
        out_specs=tuple(vmem_specs(2)),
    )(block_list, causal, queries, out_grad, kv_own, kv_near, *kv_far)

    stats_next = from_behind(stats, "ctx", -1)
    stats_far = [from_behind(stats, "ctx", -distance) for distance in distances]

    k_kernel, _ = key_side(blocks_here, entries, head_size, scale)
    key_grad, value_grad = pl.pallas_call(
        k_kernel,
        out_shape=(
            jax.ShapeDtypeStruct((tok_rows, feat), jnp.bfloat16),
            jax.ShapeDtypeStruct((tok_rows, feat), jnp.bfloat16),
        ),
        in_specs=smem_specs(2) + vmem_specs(5 + 2 * len(qg_far)),
        out_specs=tuple(vmem_specs(2)),
    )(block_list, causal, kv_own, qg_own, qg_next, stats, stats_next, *qg_far, *stats_far)
    return (query_grad, key_grad, value_grad)


def solution(mesh):
    return jax.shard_map(
        on_device,
        mesh=mesh,
        in_specs=(
            P(("dp", "ctx"), None),
            P(("dp", "ctx"), None),
            P(("dp", "ctx"), None),
            P(("dp", "ctx"), None),
            P(("dp", "ctx"), None),
            P(("dp", "ctx")),
        ),
        out_specs=(P(("dp", "ctx"), None), P(("dp", "ctx"), None), P(("dp", "ctx"), None)),
        check_vma=False,
    )
```

```python
import jax
import jax.numpy as jnp
from jax import lax
from jax.experimental import pallas as pl
from jax.experimental.pallas import tpu as pltpu
from jax.sharding import PartitionSpec as P

BLOCK = 128
HEADS = 2


def from_behind(value, axis, steps):
    count = lax.axis_size(axis)
    initial, last = (max(0, -steps), min(count, count - steps))
    return lax.ppermute(value, axis, [(source, source + steps) for source in range(initial, last)])


def dot_nt(a, b):
    return lax.dot_general(a, b, (((1,), (1,)), ((), ())), preferred_element_type=jnp.float32)


def dot_tn(a, b):
    return lax.dot_general(a, b, (((0,), (0,)), ((), ())), preferred_element_type=jnp.float32)


def dot_nn(a, b):
    return lax.dot_general(a, b, (((1,), (0,)), ((), ())), preferred_element_type=jnp.float32)


def upper_mask():
    rows = lax.broadcasted_iota(jnp.int32, (BLOCK, BLOCK), 0)
    cols = lax.broadcasted_iota(jnp.int32, (BLOCK, BLOCK), 1)
    return rows <= cols


def make_levels(blocks_here, entries):
    kinds = []
    for level in range(entries):
        reach = 2 ** (level - 1) if level > 0 else 0
        kinds.append((level, reach, "own" if level == 0 else ("near" if reach <= blocks_here else "far")))
    return kinds


def query_side(blocks_here, entries, head_size, scale):
    kinds = make_levels(blocks_here, entries)
    far_levels = [level for level, _, kind in kinds if kind == "far"]

    def kernel(list_ref, causal_ref, q_ref, g_ref, own_ref, near_ref, *rest):
        far_refs = dict(zip(far_levels, rest[: len(far_levels)]))
        dq_ref, stats_ref = rest[len(far_levels):]
        upper = upper_mask()
        for block in range(blocks_here):
            rows = slice(block * BLOCK, (block + 1) * BLOCK)
            valid = [list_ref[block, level] >= 0 for level in range(entries)]
            self_ok = jnp.logical_or(upper, causal_ref[block] == 0)
            for head in range(HEADS):
                kcols = slice(head * head_size, (head + 1) * head_size)
                vcols = slice((HEADS + head) * head_size, (HEADS + head + 1) * head_size)
                q = q_ref[rows, kcols]
                g = g_ref[rows, kcols]
                keys_at = []
                values_at = []
                for level, reach, kind in kinds:
                    if kind == "own":
                        src, at = own_ref, block
                    elif kind == "near":
                        joined = blocks_here + block - reach
                        src, at = (own_ref, joined - blocks_here) if joined >= blocks_here else (near_ref, joined)
                    else:
                        src, at = far_refs[level], block
                    keys_at.append(src[at * BLOCK : (at + 1) * BLOCK, kcols])
                    values_at.append(src[at * BLOCK : (at + 1) * BLOCK, vcols])
                scores = []
                for level in range(entries):
                    s = dot_nt(keys_at[level], q) * scale
                    keep = jnp.logical_and(self_ok, valid[0]) if level == 0 else valid[level]
                    scores.append(jnp.where(keep, s, -jnp.inf))
                top = scores[0].max(axis=0, keepdims=True)
                for level in range(1, entries):
                    top = jnp.maximum(top, scores[level].max(axis=0, keepdims=True))
                total = jnp.zeros_like(top)
                for level in range(entries):
                    total = total + jnp.sum(jnp.exp(scores[level] - top), axis=0, keepdims=True)
                lse = top + jnp.log(total)
                probs = []
                dprobs = []
                delta = jnp.zeros_like(top)
                for level in range(entries):
                    p = jnp.exp(scores[level] - lse)
                    dp = dot_nt(values_at[level], g)
                    w = p.astype(jnp.bfloat16).astype(jnp.float32)
                    delta = delta + jnp.sum(w * dp, axis=0, keepdims=True)
                    probs.append(p)
                    dprobs.append(dp)
                dq = jnp.zeros((BLOCK, head_size), jnp.float32)
                for level in range(entries):
                    ds = (probs[level] * (dprobs[level] - delta)).astype(jnp.bfloat16)
                    dq = dq + dot_tn(ds, keys_at[level])
                dq_ref[rows, kcols] = (dq * scale).astype(dq_ref.dtype)
                stats_ref[head : head + 1, rows] = delta
                for level in range(entries):
                    row = HEADS + HEADS * level + head
                    stats_ref[row : row + 1, rows] = jnp.where(valid[level], lse, jnp.inf)

    return kernel, far_levels


def key_side(blocks_here, entries, head_size, scale, devices):
    kinds = make_levels(blocks_here, entries)
    far_levels = [level for level, _, kind in kinds if kind == "far"]

    def kernel(list_ref, causal_ref, place_ref, kv_ref, qg_ref, qg_next_ref, stats_ref, *rest):
        count = len(far_levels)
        far_qg = dict(zip(far_levels, rest[:count]))
        dk_ref, dv_ref = rest[count:]
        upper = upper_mask()
        place = place_ref[0]
        for block in range(blocks_here):
            rows = slice(block * BLOCK, (block + 1) * BLOCK)
            self_ok = jnp.logical_or(upper, causal_ref[block] == 0)
            for head in range(HEADS):
                kcols = slice(head * head_size, (head + 1) * head_size)
                vcols = slice((HEADS + head) * head_size, (HEADS + head + 1) * head_size)
                k = kv_ref[rows, kcols]
                v = kv_ref[rows, vcols]
                dk = jnp.zeros((BLOCK, head_size), jnp.float32)
                dv = jnp.zeros((BLOCK, head_size), jnp.float32)
                for level, reach, kind in kinds:
                    if kind == "own":
                        src, ahead, at = qg_ref, 0, block
                    elif kind == "near":
                        joined = block + reach
                        if joined < blocks_here:
                            src, ahead, at = qg_ref, 0, joined
                        else:
                            src, ahead, at = qg_next_ref, 1, joined - blocks_here
                    else:
                        src, ahead, at = far_qg[level], reach // blocks_here, block
                    qrows = slice(at * BLOCK, (at + 1) * BLOCK)
                    q = src[qrows, kcols]
                    g = src[qrows, vcols]
                    row = HEADS + HEADS * level + head
                    holder = jnp.minimum(place + ahead, devices - 1)
                    lse = stats_ref[holder, row : row + 1, qrows]
                    delta = stats_ref[holder, head : head + 1, qrows]
                    s = dot_nt(k, q) * scale
                    if kind == "own":
                        s = jnp.where(self_ok, s, -jnp.inf)
                    p = jnp.exp(s - lse)
                    if ahead > 0:
                        p = jnp.where(place + ahead < devices, p, 0.0)
                    w = p.astype(jnp.bfloat16)
                    dp = dot_nt(v, g)
                    ds = (p * (dp - delta)).astype(jnp.bfloat16)
                    dk = dk + dot_nn(ds, q)
                    dv = dv + dot_nn(w, g)
                dk_ref[rows, kcols] = (dk * scale).astype(dk_ref.dtype)
                dv_ref[rows, kcols] = dv.astype(dv_ref.dtype)

    return kernel, far_levels


def vmem_specs(count):
    return [pl.BlockSpec(memory_space=pltpu.VMEM) for _ in range(count)]


def smem_specs(count):
    return [pl.BlockSpec(memory_space=pltpu.SMEM) for _ in range(count)]


def on_device(queries, keys, values, out_grad, block_list, causal):
    tok_rows, feat = queries.shape
    blocks_here = tok_rows // BLOCK
    entries = block_list.shape[1]
    head_size = feat // HEADS
    scale = head_size ** (-0.5)
    stat_cols = HEADS + HEADS * entries

    kv_own = jnp.concatenate([keys, values], 1)
    qg_own = jnp.concatenate([queries, out_grad], 1)
    kv_near = from_behind(kv_own, "ctx", 1)
    qg_next = from_behind(qg_own, "ctx", -1)
    q_kernel, far_levels = query_side(blocks_here, entries, head_size, scale)
    kv_far = []
    qg_far = []
    distances = [2 ** (level - 1) // blocks_here for level in far_levels]
    for distance in distances:
        kv_far.append(from_behind(kv_own, "ctx", distance))
        qg_far.append(from_behind(qg_own, "ctx", -distance))

    query_grad, stats = pl.pallas_call(
        q_kernel,
        out_shape=(
            jax.ShapeDtypeStruct((tok_rows, feat), jnp.bfloat16),
            jax.ShapeDtypeStruct((stat_cols, tok_rows), jnp.float32),
        ),
        in_specs=smem_specs(2) + vmem_specs(4 + len(kv_far)),
        out_specs=tuple(vmem_specs(2)),
    )(block_list, causal, queries, out_grad, kv_own, kv_near, *kv_far)

    devices = lax.axis_size("ctx")
    stats_all = lax.all_gather(stats, "ctx")
    place = lax.axis_index("ctx").astype(jnp.int32).reshape(1)

    k_kernel, _ = key_side(blocks_here, entries, head_size, scale, devices)
    key_grad, value_grad = pl.pallas_call(
        k_kernel,
        out_shape=(
            jax.ShapeDtypeStruct((tok_rows, feat), jnp.bfloat16),
            jax.ShapeDtypeStruct((tok_rows, feat), jnp.bfloat16),
        ),
        in_specs=smem_specs(3) + vmem_specs(4 + len(qg_far)),
        out_specs=tuple(vmem_specs(2)),
    )(block_list, causal, place, kv_own, qg_own, qg_next, stats_all, *qg_far)
    return (query_grad, key_grad, value_grad)


def solution(mesh):
    return jax.shard_map(
        on_device,
        mesh=mesh,
        in_specs=(
            P(("dp", "ctx"), None),
            P(("dp", "ctx"), None),
            P(("dp", "ctx"), None),
            P(("dp", "ctx"), None),
            P(("dp", "ctx"), None),
            P(("dp", "ctx")),
        ),
        out_specs=(P(("dp", "ctx"), None), P(("dp", "ctx"), None), P(("dp", "ctx"), None)),
        check_vma=False,
    )
```

```python
import jax
import jax.numpy as jnp
from jax import lax
from jax.experimental import pallas as pl
from jax.experimental.pallas import tpu as pltpu
from jax.sharding import PartitionSpec as P

BLOCK = 128
HEADS = 2


def from_behind(value, axis, steps):
    count = lax.axis_size(axis)
    initial, last = (max(0, -steps), min(count, count - steps))
    return lax.ppermute(value, axis, [(source, source + steps) for source in range(initial, last)])


def dot_nt(a, b):
    return lax.dot_general(a, b, (((1,), (1,)), ((), ())), preferred_element_type=jnp.float32)


def dot_tn(a, b):
    return lax.dot_general(a, b, (((0,), (0,)), ((), ())), preferred_element_type=jnp.float32)


def dot_nn(a, b):
    return lax.dot_general(a, b, (((1,), (0,)), ((), ())), preferred_element_type=jnp.float32)


def upper_mask():
    rows = lax.broadcasted_iota(jnp.int32, (BLOCK, BLOCK), 0)
    cols = lax.broadcasted_iota(jnp.int32, (BLOCK, BLOCK), 1)
    return rows <= cols


def make_levels(blocks_here, entries):
    kinds = []
    for level in range(entries):
        reach = 2 ** (level - 1) if level > 0 else 0
        kinds.append((level, reach, "own" if level == 0 else ("near" if reach <= blocks_here else "far")))
    return kinds


def query_side(blocks_here, entries, head_size, scale):
    kinds = make_levels(blocks_here, entries)
    far_levels = [level for level, _, kind in kinds if kind == "far"]

    def kernel(list_ref, causal_ref, q_ref, g_ref, own_ref, near_ref, *rest):
        far_refs = dict(zip(far_levels, rest[: len(far_levels)]))
        dq_ref, stats_ref = rest[len(far_levels):]
        upper = upper_mask()
        for block in range(blocks_here):
            rows = slice(block * BLOCK, (block + 1) * BLOCK)
            valid = [list_ref[block, level] >= 0 for level in range(entries)]
            self_ok = jnp.logical_or(upper, causal_ref[block] == 0)
            for head in range(HEADS):
                kcols = slice(head * head_size, (head + 1) * head_size)
                vcols = slice((HEADS + head) * head_size, (HEADS + head + 1) * head_size)
                q = q_ref[rows, kcols]
                g = g_ref[rows, kcols]
                keys_at = []
                values_at = []
                for level, reach, kind in kinds:
                    if kind == "own":
                        src, at = own_ref, block
                    elif kind == "near":
                        joined = blocks_here + block - reach
                        src, at = (own_ref, joined - blocks_here) if joined >= blocks_here else (near_ref, joined)
                    else:
                        src, at = far_refs[level], block
                    keys_at.append(src[at * BLOCK : (at + 1) * BLOCK, kcols])
                    values_at.append(src[at * BLOCK : (at + 1) * BLOCK, vcols])
                scores = []
                for level in range(entries):
                    s = dot_nt(keys_at[level], q) * scale
                    keep = jnp.logical_and(self_ok, valid[0]) if level == 0 else valid[level]
                    scores.append(jnp.where(keep, s, -jnp.inf))
                top = scores[0].max(axis=0, keepdims=True)
                for level in range(1, entries):
                    top = jnp.maximum(top, scores[level].max(axis=0, keepdims=True))
                total = jnp.zeros_like(top)
                for level in range(entries):
                    total = total + jnp.sum(jnp.exp(scores[level] - top), axis=0, keepdims=True)
                lse = top + jnp.log(total)
                probs = []
                dprobs = []
                delta = jnp.zeros_like(top)
                for level in range(entries):
                    p = jnp.exp(scores[level] - lse)
                    dp = dot_nt(values_at[level], g)
                    w = p.astype(jnp.bfloat16).astype(jnp.float32)
                    delta = delta + jnp.sum(w * dp, axis=0, keepdims=True)
                    probs.append(p)
                    dprobs.append(dp)
                dq = jnp.zeros((BLOCK, head_size), jnp.float32)
                for level in range(entries):
                    ds = (probs[level] * (dprobs[level] - delta)).astype(jnp.bfloat16)
                    dq = dq + dot_tn(ds, keys_at[level])
                dq_ref[rows, kcols] = (dq * scale).astype(dq_ref.dtype)
                stats_ref[head : head + 1, rows] = delta
                for level in range(entries):
                    row = HEADS + HEADS * level + head
                    stats_ref[row : row + 1, rows] = jnp.where(valid[level], lse, jnp.inf)

    return kernel, far_levels


def key_side(blocks_here, entries, head_size, scale):
    kinds = make_levels(blocks_here, entries)
    far_levels = [level for level, _, kind in kinds if kind == "far"]

    def kernel(list_ref, causal_ref, kv_ref, qg_ref, qg_next_ref, stats_ref, stats_next_ref, *rest):
        count = len(far_levels)
        far_qg = dict(zip(far_levels, rest[:count]))
        far_stats = dict(zip(far_levels, rest[count : 2 * count]))
        dk_ref, dv_ref = rest[2 * count :]
        upper = upper_mask()
        for block in range(blocks_here):
            rows = slice(block * BLOCK, (block + 1) * BLOCK)
            self_ok = jnp.logical_or(upper, causal_ref[block] == 0)
            for head in range(HEADS):
                kcols = slice(head * head_size, (head + 1) * head_size)
                vcols = slice((HEADS + head) * head_size, (HEADS + head + 1) * head_size)
                k = kv_ref[rows, kcols]
                v = kv_ref[rows, vcols]
                dk = jnp.zeros((BLOCK, head_size), jnp.float32)
                dv = jnp.zeros((BLOCK, head_size), jnp.float32)
                for level, reach, kind in kinds:
                    if kind == "own":
                        src, st, at = qg_ref, stats_ref, block
                    elif kind == "near":
                        joined = block + reach
                        if joined < blocks_here:
                            src, st, at = qg_ref, stats_ref, joined
                        else:
                            src, st, at = qg_next_ref, stats_next_ref, joined - blocks_here
                    else:
                        src, st, at = far_qg[level], far_stats[level], block
                    qrows = slice(at * BLOCK, (at + 1) * BLOCK)
                    q = src[qrows, kcols]
                    g = src[qrows, vcols]
                    row = HEADS + HEADS * level + head
                    lse = st[row : row + 1, qrows]
                    delta = st[head : head + 1, qrows]
                    s = dot_nt(k, q) * scale
                    if kind == "own":
                        s = jnp.where(self_ok, s, -jnp.inf)
                    p = jnp.exp(s - lse)
                    w = p.astype(jnp.bfloat16)
                    dp = dot_nt(v, g)
                    ds = (p * (dp - delta)).astype(jnp.bfloat16)
                    dk = dk + dot_nn(ds, q)
                    dv = dv + dot_nn(w, g)
                dk_ref[rows, kcols] = (dk * scale).astype(dk_ref.dtype)
                dv_ref[rows, kcols] = dv.astype(dv_ref.dtype)

    return kernel, far_levels


def vmem_specs(count):
    return [pl.BlockSpec(memory_space=pltpu.VMEM) for _ in range(count)]


def smem_specs(count):
    return [pl.BlockSpec(memory_space=pltpu.SMEM) for _ in range(count)]


def on_device(queries, keys, values, out_grad, block_list, causal):
    tok_rows, feat = queries.shape
    blocks_here = tok_rows // BLOCK
    entries = block_list.shape[1]
    head_size = feat // HEADS
    scale = head_size ** (-0.5)
    stat_cols = HEADS + HEADS * entries

    kv_own = jnp.concatenate([keys, values], 1)
    qg_own = jnp.concatenate([queries, out_grad], 1)
    kv_near = from_behind(kv_own, "ctx", 1)
    qg_next = from_behind(qg_own, "ctx", -1)
    q_kernel, far_levels = query_side(blocks_here, entries, head_size, scale)
    kv_far = []
    qg_far = []
    distances = [2 ** (level - 1) // blocks_here for level in far_levels]
    for distance in distances:
        kv_far.append(from_behind(kv_own, "ctx", distance))
        qg_far.append(from_behind(qg_own, "ctx", -distance))

    query_grad, stats = pl.pallas_call(
        q_kernel,
        out_shape=(
            jax.ShapeDtypeStruct((tok_rows, feat), jnp.bfloat16),
            jax.ShapeDtypeStruct((stat_cols, tok_rows), jnp.float32),
        ),
        in_specs=smem_specs(2) + vmem_specs(4 + len(kv_far)),
        out_specs=tuple(vmem_specs(2)),
    )(block_list, causal, queries, out_grad, kv_own, kv_near, *kv_far)

    stats_next = from_behind(stats, "ctx", -1)
    stats_far = [from_behind(stats, "ctx", -distance) for distance in distances]

    k_kernel, _ = key_side(blocks_here, entries, head_size, scale)
    key_grad, value_grad = pl.pallas_call(
        k_kernel,
        out_shape=(
            jax.ShapeDtypeStruct((tok_rows, feat), jnp.bfloat16),
            jax.ShapeDtypeStruct((tok_rows, feat), jnp.bfloat16),
        ),
        in_specs=smem_specs(2) + vmem_specs(5 + 2 * len(qg_far)),
        out_specs=tuple(vmem_specs(2)),
    )(block_list, causal, kv_own, qg_own, qg_next, stats, stats_next, *qg_far, *stats_far)
    return (query_grad, key_grad, value_grad)


def solution(mesh):
    return jax.shard_map(
        on_device,
        mesh=mesh,
        in_specs=(
            P(("dp", "ctx"), None),
            P(("dp", "ctx"), None),
            P(("dp", "ctx"), None),
            P(("dp", "ctx"), None),
            P(("dp", "ctx"), None),
            P(("dp", "ctx")),
        ),
        out_specs=(P(("dp", "ctx"), None), P(("dp", "ctx"), None), P(("dp", "ctx"), None)),
        check_vma=False,
    )
```

```python
import jax
import jax.numpy as jnp
from jax import lax
from jax.experimental import pallas as pl
from jax.experimental.pallas import tpu as pltpu
from jax.sharding import PartitionSpec as P

BLOCK = 128
HEADS = 2


def from_behind(value, axis, steps):
    count = lax.axis_size(axis)
    initial, last = (max(0, -steps), min(count, count - steps))
    return lax.ppermute(value, axis, [(source, source + steps) for source in range(initial, last)])


def dot_nt(a, b):
    return lax.dot_general(a, b, (((1,), (1,)), ((), ())), preferred_element_type=jnp.float32)


def dot_tn(a, b):
    return lax.dot_general(a, b, (((0,), (0,)), ((), ())), preferred_element_type=jnp.float32)


def dot_nn(a, b):
    return lax.dot_general(a, b, (((1,), (0,)), ((), ())), preferred_element_type=jnp.float32)


def behind(parity, pair, rows, cols):
    return jnp.where(parity == 0, pair[1][rows, cols], pair[0][rows, cols])


def ahead(parity, pair, rows, cols):
    return jnp.where(parity == 0, pair[0][rows, cols], pair[1][rows, cols])


def swap(lower_value, upper_value, axis, distance, group, parity):
    count = lax.axis_size(axis)
    pairs = []
    for low in range(count - distance):
        if (low // distance) % 2 == group:
            pairs += [(low, low + distance), (low + distance, low)]
    is_lower = parity == group
    operand = lower_value if upper_value is None else jnp.where(is_lower, lower_value, upper_value)
    return lax.ppermute(operand, axis, pairs)


def upper_mask():
    rows = lax.broadcasted_iota(jnp.int32, (BLOCK, BLOCK), 0)
    cols = lax.broadcasted_iota(jnp.int32, (BLOCK, BLOCK), 1)
    return rows <= cols


def make_levels(blocks_here, entries):
    kinds = []
    for level in range(entries):
        reach = 2 ** (level - 1) if level > 0 else 0
        kinds.append((level, reach, "own" if level == 0 else ("near" if reach <= blocks_here else "far")))
    return kinds


def query_side(blocks_here, entries, head_size, scale):
    kinds = make_levels(blocks_here, entries)
    far_levels = [level for level, _, kind in kinds if kind == "far"]

    def kernel(list_ref, causal_ref, parity_ref, q_ref, g_ref, own_ref, *rest):
        pairs = [rest[2 * index : 2 * index + 2] for index in range(1 + len(far_levels))]
        near_ref = pairs[0]
        far_refs = dict(zip(far_levels, pairs[1:]))
        dq_ref, stats_ref = rest[2 * len(pairs):]
        upper = upper_mask()
        slots = {level: 1 + index for index, level in enumerate(far_levels)}
        for block in range(blocks_here):
            rows = slice(block * BLOCK, (block + 1) * BLOCK)
            valid = [list_ref[block, level] >= 0 for level in range(entries)]
            self_ok = jnp.logical_or(upper, causal_ref[block] == 0)
            for head in range(HEADS):
                kcols = slice(head * head_size, (head + 1) * head_size)
                vcols = slice((HEADS + head) * head_size, (HEADS + head + 1) * head_size)
                q = q_ref[rows, kcols]
                g = g_ref[rows, kcols]
                keys_at = []
                values_at = []
                for level, reach, kind in kinds:
                    if kind == "own":
                        src, slot, at = own_ref, None, block
                    elif kind == "near":
                        joined = blocks_here + block - reach
                        if joined >= blocks_here:
                            src, slot, at = own_ref, None, joined - blocks_here
                        else:
                            src, slot, at = near_ref, 0, joined
                    else:
                        src, slot, at = far_refs[level], slots[level], block
                    krows = slice(at * BLOCK, (at + 1) * BLOCK)
                    if slot is None:
                        keys_at.append(src[krows, kcols])
                        values_at.append(src[krows, vcols])
                    else:
                        keys_at.append(behind(parity_ref[slot], src, krows, kcols))
                        values_at.append(behind(parity_ref[slot], src, krows, vcols))
                scores = []
                for level in range(entries):
                    s = dot_nt(keys_at[level], q) * scale
                    keep = jnp.logical_and(self_ok, valid[0]) if level == 0 else valid[level]
                    scores.append(jnp.where(keep, s, -jnp.inf))
                top = scores[0].max(axis=0, keepdims=True)
                for level in range(1, entries):
                    top = jnp.maximum(top, scores[level].max(axis=0, keepdims=True))
                total = jnp.zeros_like(top)
                for level in range(entries):
                    total = total + jnp.sum(jnp.exp(scores[level] - top), axis=0, keepdims=True)
                lse = top + jnp.log(total)
                probs = []
                dprobs = []
                delta = jnp.zeros_like(top)
                for level in range(entries):
                    p = jnp.exp(scores[level] - lse)
                    dp = dot_nt(values_at[level], g)
                    w = p.astype(jnp.bfloat16).astype(jnp.float32)
                    delta = delta + jnp.sum(w * dp, axis=0, keepdims=True)
                    probs.append(p)
                    dprobs.append(dp)
                dq = jnp.zeros((BLOCK, head_size), jnp.float32)
                for level in range(entries):
                    ds = (probs[level] * (dprobs[level] - delta)).astype(jnp.bfloat16)
                    dq = dq + dot_tn(ds, keys_at[level])
                dq_ref[rows, kcols] = (dq * scale).astype(dq_ref.dtype)
                stats_ref[head : head + 1, rows] = delta
                for level in range(entries):
                    row = HEADS + HEADS * level + head
                    stats_ref[row : row + 1, rows] = jnp.where(valid[level], lse, jnp.inf)

    return kernel, far_levels


def key_side(blocks_here, entries, head_size, scale):
    kinds = make_levels(blocks_here, entries)
    far_levels = [level for level, _, kind in kinds if kind == "far"]

    def kernel(list_ref, causal_ref, parity_ref, kv_ref, qg_ref, stats_ref, *rest):
        count = 1 + len(far_levels)
        qg_pairs = [rest[2 * index : 2 * index + 2] for index in range(count)]
        stat_pairs = [rest[2 * (count + index) : 2 * (count + index) + 2] for index in range(count)]
        dk_ref, dv_ref = rest[4 * count :]
        slots = {level: 1 + index for index, level in enumerate(far_levels)}
        upper = upper_mask()
        for block in range(blocks_here):
            rows = slice(block * BLOCK, (block + 1) * BLOCK)
            self_ok = jnp.logical_or(upper, causal_ref[block] == 0)
            for head in range(HEADS):
                kcols = slice(head * head_size, (head + 1) * head_size)
                vcols = slice((HEADS + head) * head_size, (HEADS + head + 1) * head_size)
                k = kv_ref[rows, kcols]
                v = kv_ref[rows, vcols]
                dk = jnp.zeros((BLOCK, head_size), jnp.float32)
                dv = jnp.zeros((BLOCK, head_size), jnp.float32)
                for level, reach, kind in kinds:
                    if kind == "own":
                        slot, at = None, block
                    elif kind == "near":
                        joined = block + reach
                        slot, at = (None, joined) if joined < blocks_here else (0, joined - blocks_here)
                    else:
                        slot, at = slots[level], block
                    qrows = slice(at * BLOCK, (at + 1) * BLOCK)
                    row = HEADS + HEADS * level + head
                    if slot is None:
                        q = qg_ref[qrows, kcols]
                        g = qg_ref[qrows, vcols]
                        lse = stats_ref[row : row + 1, qrows]
                        delta = stats_ref[head : head + 1, qrows]
                    else:
                        parity = parity_ref[slot]
                        q = ahead(parity, qg_pairs[slot], qrows, kcols)
                        g = ahead(parity, qg_pairs[slot], qrows, vcols)
                        lse = ahead(parity, stat_pairs[slot], slice(row, row + 1), qrows)
                        delta = ahead(parity, stat_pairs[slot], slice(head, head + 1), qrows)
                    s = dot_nt(k, q) * scale
                    if kind == "own":
                        s = jnp.where(self_ok, s, -jnp.inf)
                    p = jnp.exp(s - lse)
                    w = p.astype(jnp.bfloat16)
                    dp = dot_nt(v, g)
                    ds = (p * (dp - delta)).astype(jnp.bfloat16)
                    dk = dk + dot_nn(ds, q)
                    dv = dv + dot_nn(w, g)
                dk_ref[rows, kcols] = (dk * scale).astype(dk_ref.dtype)
                dv_ref[rows, kcols] = dv.astype(dv_ref.dtype)

    return kernel, far_levels


def vmem_specs(count):
    return [pl.BlockSpec(memory_space=pltpu.VMEM) for _ in range(count)]


def smem_specs(count):
    return [pl.BlockSpec(memory_space=pltpu.SMEM) for _ in range(count)]


def on_device(queries, keys, values, out_grad, block_list, causal):
    tok_rows, feat = queries.shape
    blocks_here = tok_rows // BLOCK
    entries = block_list.shape[1]
    head_size = feat // HEADS
    scale = head_size ** (-0.5)
    stat_cols = HEADS + HEADS * entries

    kv_own = jnp.concatenate([keys, values], 1)
    qg_own = jnp.concatenate([queries, out_grad], 1)
    q_kernel, far_levels = query_side(blocks_here, entries, head_size, scale)
    distances = [1] + [2 ** (level - 1) // blocks_here for level in far_levels]
    place = lax.axis_index("ctx")
    parities = [(place // distance) % 2 for distance in distances]
    parity = jnp.stack(parities).astype(jnp.int32)
    kv_pairs = []
    for distance, side in zip(distances, parities):
        kv_pairs += [swap(kv_own, qg_own, "ctx", distance, group, side) for group in range(2)]

    query_grad, stats = pl.pallas_call(
        q_kernel,
        out_shape=(
            jax.ShapeDtypeStruct((tok_rows, feat), jnp.bfloat16),
            jax.ShapeDtypeStruct((stat_cols, tok_rows), jnp.float32),
        ),
        in_specs=smem_specs(3) + vmem_specs(3 + len(kv_pairs)),
        out_specs=tuple(vmem_specs(2)),
    )(block_list, causal, parity, queries, out_grad, kv_own, *kv_pairs)

    stat_pairs = []
    for distance, side in zip(distances, parities):
        stat_pairs += [swap(stats, None, "ctx", distance, group, side) for group in range(2)]

    k_kernel, _ = key_side(blocks_here, entries, head_size, scale)
    key_grad, value_grad = pl.pallas_call(
        k_kernel,
        out_shape=(
            jax.ShapeDtypeStruct((tok_rows, feat), jnp.bfloat16),
            jax.ShapeDtypeStruct((tok_rows, feat), jnp.bfloat16),
        ),
        in_specs=smem_specs(3) + vmem_specs(3 + 2 * len(kv_pairs)),
        out_specs=tuple(vmem_specs(2)),
    )(block_list, causal, parity, kv_own, qg_own, stats, *kv_pairs, *stat_pairs)
    return (query_grad, key_grad, value_grad)


def solution(mesh):
    return jax.shard_map(
        on_device,
        mesh=mesh,
        in_specs=(
            P(("dp", "ctx"), None),
            P(("dp", "ctx"), None),
            P(("dp", "ctx"), None),
            P(("dp", "ctx"), None),
            P(("dp", "ctx"), None),
            P(("dp", "ctx")),
        ),
        out_specs=(P(("dp", "ctx"), None), P(("dp", "ctx"), None), P(("dp", "ctx"), None)),
        check_vma=False,
    )
```

```python
import jax
import jax.numpy as jnp
from jax import lax
from jax.experimental import pallas as pl
from jax.experimental.pallas import tpu as pltpu
from jax.sharding import PartitionSpec as P

BLOCK = 128
HEADS = 2


def from_behind(value, axis, steps):
    count = lax.axis_size(axis)
    initial, last = (max(0, -steps), min(count, count - steps))
    return lax.ppermute(value, axis, [(source, source + steps) for source in range(initial, last)])


def dot_nt(a, b):
    return lax.dot_general(a, b, (((1,), (1,)), ((), ())), preferred_element_type=jnp.float32)


def dot_tn(a, b):
    return lax.dot_general(a, b, (((0,), (0,)), ((), ())), preferred_element_type=jnp.float32)


def dot_nn(a, b):
    return lax.dot_general(a, b, (((1,), (0,)), ((), ())), preferred_element_type=jnp.float32)


def upper_mask():
    rows = lax.broadcasted_iota(jnp.int32, (BLOCK, BLOCK), 0)
    cols = lax.broadcasted_iota(jnp.int32, (BLOCK, BLOCK), 1)
    return rows <= cols


def make_levels(blocks_here, entries):
    kinds = []
    for level in range(entries):
        reach = 2 ** (level - 1) if level > 0 else 0
        kinds.append((level, reach, "own" if level == 0 else ("near" if reach <= blocks_here else "far")))
    return kinds


def query_side(blocks_here, entries, head_size, scale):
    kinds = make_levels(blocks_here, entries)
    far_levels = [level for level, _, kind in kinds if kind == "far"]

    def kernel(list_ref, causal_ref, q_ref, g_ref, own_ref, near_ref, *rest):
        count = len(far_levels)
        far_refs = dict(zip(far_levels, rest[:count]))
        dq_ref, stats_ref = rest[count : count + 2]
        term_refs = dict(zip(far_levels, rest[count + 2 :]))
        upper = upper_mask()
        for block in range(blocks_here):
            rows = slice(block * BLOCK, (block + 1) * BLOCK)
            valid = [list_ref[block, level] >= 0 for level in range(entries)]
            self_ok = jnp.logical_or(upper, causal_ref[block] == 0)
            for head in range(HEADS):
                kcols = slice(head * head_size, (head + 1) * head_size)
                vcols = slice((HEADS + head) * head_size, (HEADS + head + 1) * head_size)
                q = q_ref[rows, kcols]
                g = g_ref[rows, kcols]
                keys_at = []
                values_at = []
                for level, reach, kind in kinds:
                    if kind == "own":
                        src, at = own_ref, block
                    elif kind == "near":
                        joined = blocks_here + block - reach
                        src, at = (own_ref, joined - blocks_here) if joined >= blocks_here else (near_ref, joined)
                    else:
                        src, at = far_refs[level], block
                    keys_at.append(src[at * BLOCK : (at + 1) * BLOCK, kcols])
                    values_at.append(src[at * BLOCK : (at + 1) * BLOCK, vcols])
                scores = []
                for level in range(entries):
                    s = dot_nt(keys_at[level], q) * scale
                    keep = jnp.logical_and(self_ok, valid[0]) if level == 0 else valid[level]
                    scores.append(jnp.where(keep, s, -jnp.inf))
                top = scores[0].max(axis=0, keepdims=True)
                for level in range(1, entries):
                    top = jnp.maximum(top, scores[level].max(axis=0, keepdims=True))
                total = jnp.zeros_like(top)
                for level in range(entries):
                    total = total + jnp.sum(jnp.exp(scores[level] - top), axis=0, keepdims=True)
                lse = top + jnp.log(total)
                probs = []
                dprobs = []
                delta = jnp.zeros_like(top)
                for level in range(entries):
                    p = jnp.exp(scores[level] - lse)
                    dp = dot_nt(values_at[level], g)
                    w = p.astype(jnp.bfloat16).astype(jnp.float32)
                    delta = delta + jnp.sum(w * dp, axis=0, keepdims=True)
                    probs.append(p)
                    dprobs.append(dp)
                dq = jnp.zeros((BLOCK, head_size), jnp.float32)
                for level in range(entries):
                    ds = (probs[level] * (dprobs[level] - delta)).astype(jnp.bfloat16)
                    dq = dq + dot_tn(ds, keys_at[level])
                    if level in term_refs:
                        term_ref = term_refs[level]
                        term_ref[rows, kcols] = (dot_nn(ds, q) * scale).astype(term_ref.dtype)
                        w = probs[level].astype(jnp.bfloat16)
                        term_ref[rows, vcols] = dot_nn(w, g).astype(term_ref.dtype)
                dq_ref[rows, kcols] = (dq * scale).astype(dq_ref.dtype)
                stats_ref[head : head + 1, rows] = delta
                for level in range(entries):
                    row = HEADS + HEADS * level + head
                    stats_ref[row : row + 1, rows] = jnp.where(valid[level], lse, jnp.inf)

    return kernel, far_levels


def key_side(blocks_here, entries, head_size, scale):
    kinds = make_levels(blocks_here, entries)
    far_levels = [level for level, _, kind in kinds if kind == "far"]

    def kernel(list_ref, causal_ref, kv_ref, qg_ref, qg_next_ref, stats_ref, stats_next_ref, *rest):
        count = len(far_levels)
        back_refs = rest[:count]
        dk_ref, dv_ref = rest[count:]
        upper = upper_mask()
        for block in range(blocks_here):
            rows = slice(block * BLOCK, (block + 1) * BLOCK)
            self_ok = jnp.logical_or(upper, causal_ref[block] == 0)
            for head in range(HEADS):
                kcols = slice(head * head_size, (head + 1) * head_size)
                vcols = slice((HEADS + head) * head_size, (HEADS + head + 1) * head_size)
                k = kv_ref[rows, kcols]
                v = kv_ref[rows, vcols]
                dk = jnp.zeros((BLOCK, head_size), jnp.float32)
                dv = jnp.zeros((BLOCK, head_size), jnp.float32)
                back_k = jnp.zeros((BLOCK, head_size), jnp.float32)
                for back_ref in back_refs:
                    back_k = back_k + back_ref[rows, kcols].astype(jnp.float32)
                    dv = dv + back_ref[rows, vcols].astype(jnp.float32)
                for level, reach, kind in kinds:
                    if kind == "far":
                        continue
                    if kind == "own":
                        src, st, at = qg_ref, stats_ref, block
                    elif kind == "near":
                        joined = block + reach
                        if joined < blocks_here:
                            src, st, at = qg_ref, stats_ref, joined
                        else:
                            src, st, at = qg_next_ref, stats_next_ref, joined - blocks_here
                    qrows = slice(at * BLOCK, (at + 1) * BLOCK)
                    q = src[qrows, kcols]
                    g = src[qrows, vcols]
                    row = HEADS + HEADS * level + head
                    lse = st[row : row + 1, qrows]
                    delta = st[head : head + 1, qrows]
                    s = dot_nt(k, q) * scale
                    if kind == "own":
                        s = jnp.where(self_ok, s, -jnp.inf)
                    p = jnp.exp(s - lse)
                    w = p.astype(jnp.bfloat16)
                    dp = dot_nt(v, g)
                    ds = (p * (dp - delta)).astype(jnp.bfloat16)
                    dk = dk + dot_nn(ds, q)
                    dv = dv + dot_nn(w, g)
                dk_ref[rows, kcols] = (dk * scale + back_k).astype(dk_ref.dtype)
                dv_ref[rows, kcols] = dv.astype(dv_ref.dtype)

    return kernel, far_levels


def vmem_specs(count):
    return [pl.BlockSpec(memory_space=pltpu.VMEM) for _ in range(count)]


def smem_specs(count):
    return [pl.BlockSpec(memory_space=pltpu.SMEM) for _ in range(count)]


def on_device(queries, keys, values, out_grad, block_list, causal):
    tok_rows, feat = queries.shape
    blocks_here = tok_rows // BLOCK
    entries = block_list.shape[1]
    head_size = feat // HEADS
    scale = head_size ** (-0.5)
    stat_cols = HEADS + HEADS * entries

    kv_own = jnp.concatenate([keys, values], 1)
    qg_own = jnp.concatenate([queries, out_grad], 1)
    kv_near = from_behind(kv_own, "ctx", 1)
    qg_next = from_behind(qg_own, "ctx", -1)
    q_kernel, far_levels = query_side(blocks_here, entries, head_size, scale)
    distances = [2 ** (level - 1) // blocks_here for level in far_levels]
    kv_far = [from_behind(kv_own, "ctx", distance) for distance in distances]

    query_grad, stats, *terms = pl.pallas_call(
        q_kernel,
        out_shape=(
            jax.ShapeDtypeStruct((tok_rows, feat), jnp.bfloat16),
            jax.ShapeDtypeStruct((stat_cols, tok_rows), jnp.float32),
        )
        + tuple(jax.ShapeDtypeStruct((tok_rows, 2 * feat), jnp.bfloat16) for _ in far_levels),
        in_specs=smem_specs(2) + vmem_specs(4 + len(kv_far)),
        out_specs=tuple(vmem_specs(2 + len(far_levels))),
    )(block_list, causal, queries, out_grad, kv_own, kv_near, *kv_far)

    stats_next = from_behind(stats, "ctx", -1)
    terms_back = [from_behind(term, "ctx", -distance) for term, distance in zip(terms, distances)]

    k_kernel, _ = key_side(blocks_here, entries, head_size, scale)
    key_grad, value_grad = pl.pallas_call(
        k_kernel,
        out_shape=(
            jax.ShapeDtypeStruct((tok_rows, feat), jnp.bfloat16),
            jax.ShapeDtypeStruct((tok_rows, feat), jnp.bfloat16),
        ),
        in_specs=smem_specs(2) + vmem_specs(5 + len(terms_back)),
        out_specs=tuple(vmem_specs(2)),
    )(block_list, causal, kv_own, qg_own, qg_next, stats, stats_next, *terms_back)
    return (query_grad, key_grad, value_grad)


def solution(mesh):
    return jax.shard_map(
        on_device,
        mesh=mesh,
        in_specs=(
            P(("dp", "ctx"), None),
            P(("dp", "ctx"), None),
            P(("dp", "ctx"), None),
            P(("dp", "ctx"), None),
            P(("dp", "ctx"), None),
            P(("dp", "ctx")),
        ),
        out_specs=(P(("dp", "ctx"), None), P(("dp", "ctx"), None), P(("dp", "ctx"), None)),
        check_vma=False,
    )
```

```python
import jax
import jax.numpy as jnp
from jax import lax
from jax.experimental import pallas as pl
from jax.experimental.pallas import tpu as pltpu
from jax.sharding import PartitionSpec as P

BLOCK = 128
HEADS = 2


def from_behind(value, axis, steps):
    count = lax.axis_size(axis)
    initial, last = (max(0, -steps), min(count, count - steps))
    return lax.ppermute(value, axis, [(source, source + steps) for source in range(initial, last)])


def dot_nt(a, b):
    return lax.dot_general(a, b, (((1,), (1,)), ((), ())), preferred_element_type=jnp.float32)


def dot_tn(a, b):
    return lax.dot_general(a, b, (((0,), (0,)), ((), ())), preferred_element_type=jnp.float32)


def dot_nn(a, b):
    return lax.dot_general(a, b, (((1,), (0,)), ((), ())), preferred_element_type=jnp.float32)


def upper_mask():
    rows = lax.broadcasted_iota(jnp.int32, (BLOCK, BLOCK), 0)
    cols = lax.broadcasted_iota(jnp.int32, (BLOCK, BLOCK), 1)
    return rows <= cols


def make_levels(blocks_here, entries):
    kinds = []
    for level in range(entries):
        reach = 2 ** (level - 1) if level > 0 else 0
        kinds.append((level, reach, "own" if level == 0 else ("near" if reach <= blocks_here else "far")))
    return kinds


def query_side(blocks_here, entries, head_size, scale):
    kinds = make_levels(blocks_here, entries)
    far_levels = [level for level, _, kind in kinds if kind == "far"]

    def kernel(list_ref, causal_ref, q_ref, g_ref, own_ref, near_ref, *rest):
        count = len(far_levels)
        far_refs = dict(zip(far_levels, rest[:count]))
        dq_ref, stats_ref = rest[count : count + 2]
        term_refs = dict(zip(far_levels, rest[count + 2 :]))
        upper = upper_mask()
        for block in range(blocks_here):
            rows = slice(block * BLOCK, (block + 1) * BLOCK)
            valid = [list_ref[block, level] >= 0 for level in range(entries)]
            self_ok = jnp.logical_or(upper, causal_ref[block] == 0)
            for head in range(HEADS):
                kcols = slice(head * head_size, (head + 1) * head_size)
                vcols = slice((HEADS + head) * head_size, (HEADS + head + 1) * head_size)
                q = q_ref[rows, kcols]
                g = g_ref[rows, kcols]
                keys_at = []
                values_at = []
                for level, reach, kind in kinds:
                    if kind == "own":
                        src, at = own_ref, block
                    elif kind == "near":
                        joined = blocks_here + block - reach
                        src, at = (own_ref, joined - blocks_here) if joined >= blocks_here else (near_ref, joined)
                    else:
                        src, at = far_refs[level], block
                    keys_at.append(src[at * BLOCK : (at + 1) * BLOCK, kcols])
                    values_at.append(src[at * BLOCK : (at + 1) * BLOCK, vcols])
                scores = []
                for level in range(entries):
                    s = dot_nt(keys_at[level], q) * scale
                    keep = jnp.logical_and(self_ok, valid[0]) if level == 0 else valid[level]
                    scores.append(jnp.where(keep, s, -jnp.inf))
                top = scores[0].max(axis=0, keepdims=True)
                for level in range(1, entries):
                    top = jnp.maximum(top, scores[level].max(axis=0, keepdims=True))
                total = jnp.zeros_like(top)
                shifted = []
                for level in range(entries):
                    shifted.append(jnp.exp(scores[level] - top))
                    total = total + jnp.sum(shifted[level], axis=0, keepdims=True)
                lse = top + jnp.log(total)
                inverse = 1.0 / total
                probs = []
                dprobs = []
                delta = jnp.zeros_like(top)
                for level in range(entries):
                    p = shifted[level] * inverse
                    dp = dot_nt(values_at[level], g)
                    w = p.astype(jnp.bfloat16).astype(jnp.float32)
                    delta = delta + jnp.sum(w * dp, axis=0, keepdims=True)
                    probs.append(p)
                    dprobs.append(dp)
                dq = jnp.zeros((BLOCK, head_size), jnp.float32)
                for level in range(entries):
                    ds = (probs[level] * (dprobs[level] - delta)).astype(jnp.bfloat16)
                    dq = dq + dot_tn(ds, keys_at[level])
                    if level in term_refs:
                        term_ref = term_refs[level]
                        term_ref[rows, kcols] = (dot_nn(ds, q) * scale).astype(term_ref.dtype)
                        w = probs[level].astype(jnp.bfloat16)
                        term_ref[rows, vcols] = dot_nn(w, g).astype(term_ref.dtype)
                dq_ref[rows, kcols] = (dq * scale).astype(dq_ref.dtype)
                stats_ref[head : head + 1, rows] = delta
                for level in range(entries):
                    row = HEADS + HEADS * level + head
                    stats_ref[row : row + 1, rows] = jnp.where(valid[level], lse, jnp.inf)

    return kernel, far_levels


def key_side(blocks_here, entries, head_size, scale):
    kinds = make_levels(blocks_here, entries)
    far_levels = [level for level, _, kind in kinds if kind == "far"]

    def kernel(list_ref, causal_ref, kv_ref, qg_ref, qg_next_ref, stats_ref, stats_next_ref, *rest):
        count = len(far_levels)
        back_refs = rest[:count]
        dk_ref, dv_ref = rest[count:]
        upper = upper_mask()
        for block in range(blocks_here):
            rows = slice(block * BLOCK, (block + 1) * BLOCK)
            self_ok = jnp.logical_or(upper, causal_ref[block] == 0)
            for head in range(HEADS):
                kcols = slice(head * head_size, (head + 1) * head_size)
                vcols = slice((HEADS + head) * head_size, (HEADS + head + 1) * head_size)
                k = kv_ref[rows, kcols]
                v = kv_ref[rows, vcols]
                dk = jnp.zeros((BLOCK, head_size), jnp.float32)
                dv = jnp.zeros((BLOCK, head_size), jnp.float32)
                back_k = jnp.zeros((BLOCK, head_size), jnp.float32)
                for back_ref in back_refs:
                    back_k = back_k + back_ref[rows, kcols].astype(jnp.float32)
                    dv = dv + back_ref[rows, vcols].astype(jnp.float32)
                for level, reach, kind in kinds:
                    if kind == "far":
                        continue
                    if kind == "own":
                        src, st, at = qg_ref, stats_ref, block
                    elif kind == "near":
                        joined = block + reach
                        if joined < blocks_here:
                            src, st, at = qg_ref, stats_ref, joined
                        else:
                            src, st, at = qg_next_ref, stats_next_ref, joined - blocks_here
                    qrows = slice(at * BLOCK, (at + 1) * BLOCK)
                    q = src[qrows, kcols]
                    g = src[qrows, vcols]
                    row = HEADS + HEADS * level + head
                    lse = st[row : row + 1, qrows]
                    delta = st[head : head + 1, qrows]
                    s = dot_nt(k, q) * scale
                    if kind == "own":
                        s = jnp.where(self_ok, s, -jnp.inf)
                    p = jnp.exp(s - lse)
                    w = p.astype(jnp.bfloat16)
                    dp = dot_nt(v, g)
                    ds = (p * (dp - delta)).astype(jnp.bfloat16)
                    dk = dk + dot_nn(ds, q)
                    dv = dv + dot_nn(w, g)
                dk_ref[rows, kcols] = (dk * scale + back_k).astype(dk_ref.dtype)
                dv_ref[rows, kcols] = dv.astype(dv_ref.dtype)

    return kernel, far_levels


def vmem_specs(count):
    return [pl.BlockSpec(memory_space=pltpu.VMEM) for _ in range(count)]


def smem_specs(count):
    return [pl.BlockSpec(memory_space=pltpu.SMEM) for _ in range(count)]


def on_device(queries, keys, values, out_grad, block_list, causal):
    tok_rows, feat = queries.shape
    blocks_here = tok_rows // BLOCK
    entries = block_list.shape[1]
    head_size = feat // HEADS
    scale = head_size ** (-0.5)
    stat_cols = HEADS + HEADS * entries

    kv_own = jnp.concatenate([keys, values], 1)
    qg_own = jnp.concatenate([queries, out_grad], 1)
    kv_near = from_behind(kv_own, "ctx", 1)
    qg_next = from_behind(qg_own, "ctx", -1)
    q_kernel, far_levels = query_side(blocks_here, entries, head_size, scale)
    distances = [2 ** (level - 1) // blocks_here for level in far_levels]
    kv_far = [from_behind(kv_own, "ctx", distance) for distance in distances]

    query_grad, stats, *terms = pl.pallas_call(
        q_kernel,
        out_shape=(
            jax.ShapeDtypeStruct((tok_rows, feat), jnp.bfloat16),
            jax.ShapeDtypeStruct((stat_cols, tok_rows), jnp.float32),
        )
        + tuple(jax.ShapeDtypeStruct((tok_rows, 2 * feat), jnp.bfloat16) for _ in far_levels),
        in_specs=smem_specs(2) + vmem_specs(4 + len(kv_far)),
        out_specs=tuple(vmem_specs(2 + len(far_levels))),
    )(block_list, causal, queries, out_grad, kv_own, kv_near, *kv_far)

    stats_next = from_behind(stats, "ctx", -1)
    terms_back = [from_behind(term, "ctx", -distance) for term, distance in zip(terms, distances)]

    k_kernel, _ = key_side(blocks_here, entries, head_size, scale)
    key_grad, value_grad = pl.pallas_call(
        k_kernel,
        out_shape=(
            jax.ShapeDtypeStruct((tok_rows, feat), jnp.bfloat16),
            jax.ShapeDtypeStruct((tok_rows, feat), jnp.bfloat16),
        ),
        in_specs=smem_specs(2) + vmem_specs(5 + len(terms_back)),
        out_specs=tuple(vmem_specs(2)),
    )(block_list, causal, kv_own, qg_own, qg_next, stats, stats_next, *terms_back)
    return (query_grad, key_grad, value_grad)


def solution(mesh):
    return jax.shard_map(
        on_device,
        mesh=mesh,
        in_specs=(
            P(("dp", "ctx"), None),
            P(("dp", "ctx"), None),
            P(("dp", "ctx"), None),
            P(("dp", "ctx"), None),
            P(("dp", "ctx"), None),
            P(("dp", "ctx")),
        ),
        out_specs=(P(("dp", "ctx"), None), P(("dp", "ctx"), None), P(("dp", "ctx"), None)),
        check_vma=False,
    )
```

```python
import jax
import jax.numpy as jnp
from jax import lax
from jax.experimental import pallas as pl
from jax.experimental.pallas import tpu as pltpu
from jax.sharding import PartitionSpec as P

BLOCK = 128
HEADS = 2


def from_behind(value, axis, steps):
    count = lax.axis_size(axis)
    initial, last = (max(0, -steps), min(count, count - steps))
    return lax.ppermute(value, axis, [(source, source + steps) for source in range(initial, last)])


def dot_nt(a, b):
    return lax.dot_general(a, b, (((1,), (1,)), ((), ())), preferred_element_type=jnp.float32)


def dot_tn(a, b):
    return lax.dot_general(a, b, (((0,), (0,)), ((), ())), preferred_element_type=jnp.float32)


def dot_nn(a, b):
    return lax.dot_general(a, b, (((1,), (0,)), ((), ())), preferred_element_type=jnp.float32)


def upper_mask():
    rows = lax.broadcasted_iota(jnp.int32, (BLOCK, BLOCK), 0)
    cols = lax.broadcasted_iota(jnp.int32, (BLOCK, BLOCK), 1)
    return rows <= cols


def make_levels(blocks_here, entries):
    kinds = []
    for level in range(entries):
        reach = 2 ** (level - 1) if level > 0 else 0
        kinds.append((level, reach, "own" if level == 0 else ("near" if reach <= blocks_here else "far")))
    return kinds


def query_side(blocks_here, entries, head_size, scale):
    kinds = make_levels(blocks_here, entries)
    far_levels = [level for level, _, kind in kinds if kind == "far"]

    def kernel(list_ref, causal_ref, q_ref, g_ref, own_ref, near_ref, *rest):
        count = len(far_levels)
        far_refs = dict(zip(far_levels, rest[:count]))
        dq_ref, stats_ref = rest[count : count + 2]
        term_refs = dict(zip(far_levels, rest[count + 2 :]))
        upper = upper_mask()
        for block in range(blocks_here):
            rows = slice(block * BLOCK, (block + 1) * BLOCK)
            valid = [list_ref[block, level] >= 0 for level in range(entries)]
            self_ok = jnp.logical_or(upper, causal_ref[block] == 0)
            for head in range(HEADS):
                kcols = slice(head * head_size, (head + 1) * head_size)
                vcols = slice((HEADS + head) * head_size, (HEADS + head + 1) * head_size)
                q = q_ref[rows, kcols]
                g = g_ref[rows, kcols]
                keys_at = []
                values_at = []
                for level, reach, kind in kinds:
                    if kind == "own":
                        src, at = own_ref, block
                    elif kind == "near":
                        joined = blocks_here + block - reach
                        src, at = (own_ref, joined - blocks_here) if joined >= blocks_here else (near_ref, joined)
                    else:
                        src, at = far_refs[level], block
                    keys_at.append(src[at * BLOCK : (at + 1) * BLOCK, kcols])
                    values_at.append(src[at * BLOCK : (at + 1) * BLOCK, vcols])
                keys_cat = jnp.concatenate(keys_at, axis=0)
                values_cat = jnp.concatenate(values_at, axis=0)
                bias = [jnp.where(jnp.logical_and(self_ok, valid[0]), 0.0, -jnp.inf)]
                bias += [jnp.full((BLOCK, BLOCK), jnp.where(valid[level], 0.0, -jnp.inf)) for level in range(1, entries)]
                scores = dot_nt(keys_cat, q) * scale + jnp.concatenate(bias, axis=0)
                top = scores.max(axis=0, keepdims=True)
                shifted = jnp.exp(scores - top)
                total = jnp.sum(shifted, axis=0, keepdims=True)
                lse = top + jnp.log(total)
                probs = shifted * (1.0 / total)
                dprobs = dot_nt(values_cat, g)
                weights = probs.astype(jnp.bfloat16)
                delta = jnp.sum(weights.astype(jnp.float32) * dprobs, axis=0, keepdims=True)
                dscores = (probs * (dprobs - delta)).astype(jnp.bfloat16)
                dq = dot_tn(dscores, keys_cat)
                for level, term_ref in term_refs.items():
                    part = slice(level * BLOCK, (level + 1) * BLOCK)
                    term_ref[rows, kcols] = (dot_nn(dscores[part], q) * scale).astype(term_ref.dtype)
                    term_ref[rows, vcols] = dot_nn(weights[part], g).astype(term_ref.dtype)
                dq_ref[rows, kcols] = (dq * scale).astype(dq_ref.dtype)
                stats_ref[head : head + 1, rows] = delta
                for level in range(entries):
                    row = HEADS + HEADS * level + head
                    stats_ref[row : row + 1, rows] = jnp.where(valid[level], lse, jnp.inf)

    return kernel, far_levels


def key_side(blocks_here, entries, head_size, scale):
    kinds = make_levels(blocks_here, entries)
    far_levels = [level for level, _, kind in kinds if kind == "far"]

    def kernel(list_ref, causal_ref, kv_ref, qg_ref, qg_next_ref, stats_ref, stats_next_ref, *rest):
        count = len(far_levels)
        back_refs = rest[:count]
        dk_ref, dv_ref = rest[count:]
        upper = upper_mask()
        for block in range(blocks_here):
            rows = slice(block * BLOCK, (block + 1) * BLOCK)
            self_ok = jnp.logical_or(upper, causal_ref[block] == 0)
            for head in range(HEADS):
                kcols = slice(head * head_size, (head + 1) * head_size)
                vcols = slice((HEADS + head) * head_size, (HEADS + head + 1) * head_size)
                k = kv_ref[rows, kcols]
                v = kv_ref[rows, vcols]
                dk = jnp.zeros((BLOCK, head_size), jnp.float32)
                dv = jnp.zeros((BLOCK, head_size), jnp.float32)
                back_k = jnp.zeros((BLOCK, head_size), jnp.float32)
                for back_ref in back_refs:
                    back_k = back_k + back_ref[rows, kcols].astype(jnp.float32)
                    dv = dv + back_ref[rows, vcols].astype(jnp.float32)
                q_tiles, g_tiles, lse_rows, delta_rows = [], [], [], []
                for level, reach, kind in kinds:
                    if kind == "far":
                        continue
                    if kind == "own":
                        src, st, at = qg_ref, stats_ref, block
                    elif kind == "near":
                        joined = block + reach
                        if joined < blocks_here:
                            src, st, at = qg_ref, stats_ref, joined
                        else:
                            src, st, at = qg_next_ref, stats_next_ref, joined - blocks_here
                    qrows = slice(at * BLOCK, (at + 1) * BLOCK)
                    row = HEADS + HEADS * level + head
                    q_tiles.append(src[qrows, kcols])
                    g_tiles.append(src[qrows, vcols])
                    lse_rows.append(st[row : row + 1, qrows])
                    delta_rows.append(st[head : head + 1, qrows])
                q_cat = jnp.concatenate(q_tiles, axis=0)
                g_cat = jnp.concatenate(g_tiles, axis=0)
                lse = jnp.concatenate(lse_rows, axis=1)
                delta = jnp.concatenate(delta_rows, axis=1)
                bias = [jnp.where(self_ok, 0.0, -jnp.inf), jnp.zeros((BLOCK, BLOCK * (len(q_tiles) - 1)), jnp.float32)]
                s = dot_nt(k, q_cat) * scale + jnp.concatenate(bias, axis=1)
                p = jnp.exp(s - lse)
                w = p.astype(jnp.bfloat16)
                dp = dot_nt(v, g_cat)
                ds = (p * (dp - delta)).astype(jnp.bfloat16)
                dk = dk + dot_nn(ds, q_cat)
                dv = dv + dot_nn(w, g_cat)
                dk_ref[rows, kcols] = (dk * scale + back_k).astype(dk_ref.dtype)
                dv_ref[rows, kcols] = dv.astype(dv_ref.dtype)

    return kernel, far_levels


def vmem_specs(count):
    return [pl.BlockSpec(memory_space=pltpu.VMEM) for _ in range(count)]


def smem_specs(count):
    return [pl.BlockSpec(memory_space=pltpu.SMEM) for _ in range(count)]


def on_device(queries, keys, values, out_grad, block_list, causal):
    tok_rows, feat = queries.shape
    blocks_here = tok_rows // BLOCK
    entries = block_list.shape[1]
    head_size = feat // HEADS
    scale = head_size ** (-0.5)
    stat_cols = HEADS + HEADS * entries

    kv_own = jnp.concatenate([keys, values], 1)
    qg_own = jnp.concatenate([queries, out_grad], 1)
    kv_near = from_behind(kv_own, "ctx", 1)
    qg_next = from_behind(qg_own, "ctx", -1)
    q_kernel, far_levels = query_side(blocks_here, entries, head_size, scale)
    distances = [2 ** (level - 1) // blocks_here for level in far_levels]
    kv_far = [from_behind(kv_own, "ctx", distance) for distance in distances]

    query_grad, stats, *terms = pl.pallas_call(
        q_kernel,
        out_shape=(
            jax.ShapeDtypeStruct((tok_rows, feat), jnp.bfloat16),
            jax.ShapeDtypeStruct((stat_cols, tok_rows), jnp.float32),
        )
        + tuple(jax.ShapeDtypeStruct((tok_rows, 2 * feat), jnp.bfloat16) for _ in far_levels),
        in_specs=smem_specs(2) + vmem_specs(4 + len(kv_far)),
        out_specs=tuple(vmem_specs(2 + len(far_levels))),
    )(block_list, causal, queries, out_grad, kv_own, kv_near, *kv_far)

    stats_next = from_behind(stats, "ctx", -1)
    terms_back = [from_behind(term, "ctx", -distance) for term, distance in zip(terms, distances)]

    k_kernel, _ = key_side(blocks_here, entries, head_size, scale)
    key_grad, value_grad = pl.pallas_call(
        k_kernel,
        out_shape=(
            jax.ShapeDtypeStruct((tok_rows, feat), jnp.bfloat16),
            jax.ShapeDtypeStruct((tok_rows, feat), jnp.bfloat16),
        ),
        in_specs=smem_specs(2) + vmem_specs(5 + len(terms_back)),
        out_specs=tuple(vmem_specs(2)),
    )(block_list, causal, kv_own, qg_own, qg_next, stats, stats_next, *terms_back)
    return (query_grad, key_grad, value_grad)


def solution(mesh):
    return jax.shard_map(
        on_device,
        mesh=mesh,
        in_specs=(
            P(("dp", "ctx"), None),
            P(("dp", "ctx"), None),
            P(("dp", "ctx"), None),
            P(("dp", "ctx"), None),
            P(("dp", "ctx"), None),
            P(("dp", "ctx")),
        ),
        out_specs=(P(("dp", "ctx"), None), P(("dp", "ctx"), None), P(("dp", "ctx"), None)),
        check_vma=False,
    )
```

```python
import jax
import jax.numpy as jnp
from jax import lax
from jax.experimental import pallas as pl
from jax.experimental.pallas import tpu as pltpu
from jax.sharding import PartitionSpec as P

BLOCK = 128
HEADS = 2


def from_behind(value, axis, steps):
    count = lax.axis_size(axis)
    initial, last = (max(0, -steps), min(count, count - steps))
    return lax.ppermute(value, axis, [(source, source + steps) for source in range(initial, last)])


def dot_nt(a, b):
    return lax.dot_general(a, b, (((1,), (1,)), ((), ())), preferred_element_type=jnp.float32)


def dot_tn(a, b):
    return lax.dot_general(a, b, (((0,), (0,)), ((), ())), preferred_element_type=jnp.float32)


def dot_nn(a, b):
    return lax.dot_general(a, b, (((1,), (0,)), ((), ())), preferred_element_type=jnp.float32)


def upper_mask():
    rows = lax.broadcasted_iota(jnp.int32, (BLOCK, BLOCK), 0)
    cols = lax.broadcasted_iota(jnp.int32, (BLOCK, BLOCK), 1)
    return rows <= cols


def make_levels(blocks_here, entries):
    kinds = []
    for level in range(entries):
        reach = 2 ** (level - 1) if level > 0 else 0
        kinds.append((level, reach, "own" if level == 0 else ("near" if reach <= blocks_here else "far")))
    return kinds


def query_side(blocks_here, entries, head_size, scale):
    kinds = make_levels(blocks_here, entries)
    far_levels = [level for level, _, kind in kinds if kind == "far"]

    def kernel(list_ref, causal_ref, q_ref, g_ref, own_ref, near_ref, *rest):
        count = len(far_levels)
        far_refs = dict(zip(far_levels, rest[:count]))
        dq_ref, stats_ref = rest[count : count + 2]
        term_refs = dict(zip(far_levels, rest[count + 2 :]))
        upper = upper_mask()
        for block in range(blocks_here):
            rows = slice(block * BLOCK, (block + 1) * BLOCK)
            valid = [list_ref[block, level] >= 0 for level in range(entries)]
            self_ok = jnp.logical_or(upper, causal_ref[block] == 0)
            for head in range(HEADS):
                kcols = slice(head * head_size, (head + 1) * head_size)
                vcols = slice((HEADS + head) * head_size, (HEADS + head + 1) * head_size)
                q = q_ref[rows, kcols]
                g = g_ref[rows, kcols]
                keys_at = []
                values_at = []
                for level, reach, kind in kinds:
                    if kind == "own":
                        src, at = own_ref, block
                    elif kind == "near":
                        joined = blocks_here + block - reach
                        src, at = (own_ref, joined - blocks_here) if joined >= blocks_here else (near_ref, joined)
                    else:
                        src, at = far_refs[level], block
                    keys_at.append(src[at * BLOCK : (at + 1) * BLOCK, kcols])
                    values_at.append(src[at * BLOCK : (at + 1) * BLOCK, vcols])
                scores = []
                for level in range(entries):
                    s = dot_nt(keys_at[level], q) * scale
                    keep = jnp.logical_and(self_ok, valid[0]) if level == 0 else valid[level]
                    scores.append(jnp.where(keep, s, -jnp.inf))
                top = scores[0].max(axis=0, keepdims=True)
                for level in range(1, entries):
                    top = jnp.maximum(top, scores[level].max(axis=0, keepdims=True))
                total = jnp.zeros_like(top)
                shifted = []
                for level in range(entries):
                    shifted.append(jnp.exp(scores[level] - top))
                    total = total + jnp.sum(shifted[level], axis=0, keepdims=True)
                lse = top + jnp.log(total)
                inverse = 1.0 / total
                probs = []
                dprobs = []
                delta = jnp.zeros_like(top)
                for level in range(entries):
                    p = shifted[level] * inverse
                    dp = dot_nt(values_at[level], g)
                    w = p.astype(jnp.bfloat16).astype(jnp.float32)
                    delta = delta + jnp.sum(w * dp, axis=0, keepdims=True)
                    probs.append(p)
                    dprobs.append(dp)
                dq = jnp.zeros((BLOCK, head_size), jnp.float32)
                for level in range(entries):
                    ds = (probs[level] * (dprobs[level] - delta)).astype(jnp.bfloat16)
                    dq = dq + dot_tn(ds, keys_at[level])
                    if level in term_refs:
                        term_ref = term_refs[level]
                        term_ref[rows, kcols] = (dot_nn(ds, q) * scale).astype(term_ref.dtype)
                        w = probs[level].astype(jnp.bfloat16)
                        term_ref[rows, vcols] = dot_nn(w, g).astype(term_ref.dtype)
                dq_ref[rows, kcols] = (dq * scale).astype(dq_ref.dtype)
                stats_ref[head : head + 1, rows] = delta
                for level in range(entries):
                    row = HEADS + HEADS * level + head
                    stats_ref[row : row + 1, rows] = jnp.where(valid[level], lse, jnp.inf)

    return kernel, far_levels


def key_side(blocks_here, entries, head_size, scale):
    kinds = make_levels(blocks_here, entries)
    far_levels = [level for level, _, kind in kinds if kind == "far"]

    def kernel(list_ref, causal_ref, kv_ref, qg_ref, qg_next_ref, stats_ref, stats_next_ref, *rest):
        count = len(far_levels)
        back_refs = rest[:count]
        dk_ref, dv_ref = rest[count:]
        upper = upper_mask()
        for block in range(blocks_here):
            rows = slice(block * BLOCK, (block + 1) * BLOCK)
            self_ok = jnp.logical_or(upper, causal_ref[block] == 0)
            for head in range(HEADS):
                kcols = slice(head * head_size, (head + 1) * head_size)
                vcols = slice((HEADS + head) * head_size, (HEADS + head + 1) * head_size)
                k = kv_ref[rows, kcols]
                v = kv_ref[rows, vcols]
                dk = jnp.zeros((BLOCK, head_size), jnp.float32)
                dv = jnp.zeros((BLOCK, head_size), jnp.float32)
                back_k = jnp.zeros((BLOCK, head_size), jnp.float32)
                for back_ref in back_refs:
                    back_k = back_k + back_ref[rows, kcols].astype(jnp.float32)
                    dv = dv + back_ref[rows, vcols].astype(jnp.float32)
                q_tiles, g_tiles, lse_rows, delta_rows = [], [], [], []
                for level, reach, kind in kinds:
                    if kind == "far":
                        continue
                    if kind == "own":
                        src, st, at = qg_ref, stats_ref, block
                    elif kind == "near":
                        joined = block + reach
                        if joined < blocks_here:
                            src, st, at = qg_ref, stats_ref, joined
                        else:
                            src, st, at = qg_next_ref, stats_next_ref, joined - blocks_here
                    qrows = slice(at * BLOCK, (at + 1) * BLOCK)
                    row = HEADS + HEADS * level + head
                    q_tiles.append(src[qrows, kcols])
                    g_tiles.append(src[qrows, vcols])
                    lse_rows.append(st[row : row + 1, qrows])
                    delta_rows.append(st[head : head + 1, qrows])
                q_cat = jnp.concatenate(q_tiles, axis=0)
                g_cat = jnp.concatenate(g_tiles, axis=0)
                lse = jnp.concatenate(lse_rows, axis=1)
                delta = jnp.concatenate(delta_rows, axis=1)
                bias = [jnp.where(self_ok, 0.0, -jnp.inf), jnp.zeros((BLOCK, BLOCK * (len(q_tiles) - 1)), jnp.float32)]
                s = dot_nt(k, q_cat) * scale + jnp.concatenate(bias, axis=1)
                p = jnp.exp(s - lse)
                w = p.astype(jnp.bfloat16)
                dp = dot_nt(v, g_cat)
                ds = (p * (dp - delta)).astype(jnp.bfloat16)
                dk = dk + dot_nn(ds, q_cat)
                dv = dv + dot_nn(w, g_cat)
                dk_ref[rows, kcols] = (dk * scale + back_k).astype(dk_ref.dtype)
                dv_ref[rows, kcols] = dv.astype(dv_ref.dtype)

    return kernel, far_levels


def vmem_specs(count):
    return [pl.BlockSpec(memory_space=pltpu.VMEM) for _ in range(count)]


def smem_specs(count):
    return [pl.BlockSpec(memory_space=pltpu.SMEM) for _ in range(count)]


def on_device(queries, keys, values, out_grad, block_list, causal):
    tok_rows, feat = queries.shape
    blocks_here = tok_rows // BLOCK
    entries = block_list.shape[1]
    head_size = feat // HEADS
    scale = head_size ** (-0.5)
    stat_cols = HEADS + HEADS * entries

    kv_own = jnp.concatenate([keys, values], 1)
    qg_own = jnp.concatenate([queries, out_grad], 1)
    kv_near = from_behind(kv_own, "ctx", 1)
    qg_next = from_behind(qg_own, "ctx", -1)
    q_kernel, far_levels = query_side(blocks_here, entries, head_size, scale)
    distances = [2 ** (level - 1) // blocks_here for level in far_levels]
    kv_far = [from_behind(kv_own, "ctx", distance) for distance in distances]

    query_grad, stats, *terms = pl.pallas_call(
        q_kernel,
        out_shape=(
            jax.ShapeDtypeStruct((tok_rows, feat), jnp.bfloat16),
            jax.ShapeDtypeStruct((stat_cols, tok_rows), jnp.float32),
        )
        + tuple(jax.ShapeDtypeStruct((tok_rows, 2 * feat), jnp.bfloat16) for _ in far_levels),
        in_specs=smem_specs(2) + vmem_specs(4 + len(kv_far)),
        out_specs=tuple(vmem_specs(2 + len(far_levels))),
    )(block_list, causal, queries, out_grad, kv_own, kv_near, *kv_far)

    stats_next = from_behind(stats, "ctx", -1)
    terms_back = [from_behind(term, "ctx", -distance) for term, distance in zip(terms, distances)]

    k_kernel, _ = key_side(blocks_here, entries, head_size, scale)
    key_grad, value_grad = pl.pallas_call(
        k_kernel,
        out_shape=(
            jax.ShapeDtypeStruct((tok_rows, feat), jnp.bfloat16),
            jax.ShapeDtypeStruct((tok_rows, feat), jnp.bfloat16),
        ),
        in_specs=smem_specs(2) + vmem_specs(5 + len(terms_back)),
        out_specs=tuple(vmem_specs(2)),
    )(block_list, causal, kv_own, qg_own, qg_next, stats, stats_next, *terms_back)
    return (query_grad, key_grad, value_grad)


def solution(mesh):
    return jax.shard_map(
        on_device,
        mesh=mesh,
        in_specs=(
            P(("dp", "ctx"), None),
            P(("dp", "ctx"), None),
            P(("dp", "ctx"), None),
            P(("dp", "ctx"), None),
            P(("dp", "ctx"), None),
            P(("dp", "ctx")),
        ),
        out_specs=(P(("dp", "ctx"), None), P(("dp", "ctx"), None), P(("dp", "ctx"), None)),
        check_vma=False,
    )
```

```python
import jax
import jax.numpy as jnp
from jax import lax
from jax.experimental import pallas as pl
from jax.experimental.pallas import tpu as pltpu
from jax.sharding import PartitionSpec as P


BLOCK = 128
HEADS = 2


def from_behind(value, axis, steps):
    count = lax.axis_size(axis)
    initial, last = (max(0, -steps), min(count, count - steps))
    return lax.ppermute(value, axis, [(source, source + steps) for source in range(initial, last)])


def dot_nt(a, b):
    return lax.dot_general(a, b, (((1,), (1,)), ((), ())), preferred_element_type=jnp.float32)


def dot_tn(a, b):
    return lax.dot_general(a, b, (((0,), (0,)), ((), ())), preferred_element_type=jnp.float32)


def dot_nn(a, b):
    return lax.dot_general(a, b, (((1,), (0,)), ((), ())), preferred_element_type=jnp.float32)


def upper_mask():
    rows = lax.broadcasted_iota(jnp.int32, (BLOCK, BLOCK), 0)
    cols = lax.broadcasted_iota(jnp.int32, (BLOCK, BLOCK), 1)
    return rows <= cols


def make_levels(blocks_here, entries):
    kinds = []
    for level in range(entries):
        reach = 2 ** (level - 1) if level > 0 else 0
        kinds.append((level, reach, "own" if level == 0 else ("near" if reach <= blocks_here else "far")))
    return kinds


def query_side(blocks_here, entries, head_size, scale, with_grads=True):
    kinds = make_levels(blocks_here, entries)
    far_levels = [level for level, _, kind in kinds if kind == "far"]

    def kernel(list_ref, causal_ref, q_ref, g_ref, own_ref, near_ref, *rest):
        count = len(far_levels)
        far_refs = dict(zip(far_levels, rest[:count]))
        if with_grads:
            dq_ref = rest[count]
            term_refs = dict(zip(far_levels, rest[count + 1 :]))
        else:
            stats_ref = rest[count]
        upper = upper_mask()
        for block in range(blocks_here):
            rows = slice(block * BLOCK, (block + 1) * BLOCK)
            valid = [list_ref[block, level] >= 0 for level in range(entries)]
            self_ok = jnp.logical_or(upper, causal_ref[block] == 0)
            for head in range(HEADS):
                kcols = slice(head * head_size, (head + 1) * head_size)
                vcols = slice((HEADS + head) * head_size, (HEADS + head + 1) * head_size)
                q = q_ref[rows, kcols]
                g = g_ref[rows, kcols]
                keys_at = []
                values_at = []
                for level, reach, kind in kinds:
                    if kind == "own":
                        src, at = own_ref, block
                    elif kind == "near":
                        joined = blocks_here + block - reach
                        src, at = (own_ref, joined - blocks_here) if joined >= blocks_here else (near_ref, joined)
                    else:
                        src, at = far_refs[level], block
                    keys_at.append(src[at * BLOCK : (at + 1) * BLOCK, kcols])
                    values_at.append(src[at * BLOCK : (at + 1) * BLOCK, vcols])
                scores = []
                for level in range(entries):
                    s = dot_nt(keys_at[level], q) * scale
                    keep = jnp.logical_and(self_ok, valid[0]) if level == 0 else valid[level]
                    scores.append(jnp.where(keep, s, -jnp.inf))
                top = scores[0].max(axis=0, keepdims=True)
                for level in range(1, entries):
                    top = jnp.maximum(top, scores[level].max(axis=0, keepdims=True))
                total = jnp.zeros_like(top)
                shifted = []
                for level in range(entries):
                    shifted.append(jnp.exp(scores[level] - top))
                    total = total + jnp.sum(shifted[level], axis=0, keepdims=True)
                lse = top + jnp.log(total)
                inverse = 1.0 / total
                probs = []
                dprobs = []
                delta = jnp.zeros_like(top)
                for level in range(entries):
                    p = shifted[level] * inverse
                    dp = dot_nt(values_at[level], g)
                    w = p.astype(jnp.bfloat16).astype(jnp.float32)
                    delta = delta + jnp.sum(w * dp, axis=0, keepdims=True)
                    probs.append(p)
                    dprobs.append(dp)
                if not with_grads:
                    stats_ref[head : head + 1, rows] = delta
                    for level in range(entries):
                        row = HEADS + HEADS * level + head
                        stats_ref[row : row + 1, rows] = jnp.where(valid[level], lse, jnp.inf)
                    continue
                dq = jnp.zeros((BLOCK, head_size), jnp.float32)
                for level in range(entries):
                    ds = (probs[level] * (dprobs[level] - delta)).astype(jnp.bfloat16)
                    dq = dq + dot_tn(ds, keys_at[level])
                    if level in term_refs:
                        term_ref = term_refs[level]
                        term_ref[rows, kcols] = (dot_nn(ds, q) * scale).astype(term_ref.dtype)
                        w = probs[level].astype(jnp.bfloat16)
                        term_ref[rows, vcols] = dot_nn(w, g).astype(term_ref.dtype)
                dq_ref[rows, kcols] = (dq * scale).astype(dq_ref.dtype)

    return kernel, far_levels


def key_side(blocks_here, entries, head_size, scale):
    kinds = make_levels(blocks_here, entries)
    far_levels = [level for level, _, kind in kinds if kind == "far"]

    def kernel(list_ref, causal_ref, kv_ref, qg_ref, qg_next_ref, stats_ref, stats_next_ref, *rest):
        count = len(far_levels)
        back_refs = rest[:count]
        dk_ref, dv_ref = rest[count:]
        upper = upper_mask()
        for block in range(blocks_here):
            rows = slice(block * BLOCK, (block + 1) * BLOCK)
            self_ok = jnp.logical_or(upper, causal_ref[block] == 0)
            for head in range(HEADS):
                kcols = slice(head * head_size, (head + 1) * head_size)
                vcols = slice((HEADS + head) * head_size, (HEADS + head + 1) * head_size)
                k = kv_ref[rows, kcols]
                v = kv_ref[rows, vcols]
                dk = jnp.zeros((BLOCK, head_size), jnp.float32)
                dv = jnp.zeros((BLOCK, head_size), jnp.float32)
                back_k = jnp.zeros((BLOCK, head_size), jnp.float32)
                for back_ref in back_refs:
                    back_k = back_k + back_ref[rows, kcols].astype(jnp.float32)
                    dv = dv + back_ref[rows, vcols].astype(jnp.float32)
                q_tiles, g_tiles, lse_rows, delta_rows = [], [], [], []
                for level, reach, kind in kinds:
                    if kind == "far":
                        continue
                    if kind == "own":
                        src, st, at = qg_ref, stats_ref, block
                    elif kind == "near":
                        joined = block + reach
                        if joined < blocks_here:
                            src, st, at = qg_ref, stats_ref, joined
                        else:
                            src, st, at = qg_next_ref, stats_next_ref, joined - blocks_here
                    qrows = slice(at * BLOCK, (at + 1) * BLOCK)
                    row = HEADS + HEADS * level + head
                    q_tiles.append(src[qrows, kcols])
                    g_tiles.append(src[qrows, vcols])
                    lse_rows.append(st[row : row + 1, qrows])
                    delta_rows.append(st[head : head + 1, qrows])
                q_cat = jnp.concatenate(q_tiles, axis=0)
                g_cat = jnp.concatenate(g_tiles, axis=0)
                lse = jnp.concatenate(lse_rows, axis=1)
                delta = jnp.concatenate(delta_rows, axis=1)
                bias = [jnp.where(self_ok, 0.0, -jnp.inf), jnp.zeros((BLOCK, BLOCK * (len(q_tiles) - 1)), jnp.float32)]
                s = dot_nt(k, q_cat) * scale + jnp.concatenate(bias, axis=1)
                p = jnp.exp(s - lse)
                w = p.astype(jnp.bfloat16)
                dp = dot_nt(v, g_cat)
                ds = (p * (dp - delta)).astype(jnp.bfloat16)
                dk = dk + dot_nn(ds, q_cat)
                dv = dv + dot_nn(w, g_cat)
                dk_ref[rows, kcols] = (dk * scale + back_k).astype(dk_ref.dtype)
                dv_ref[rows, kcols] = dv.astype(dv_ref.dtype)

    return kernel, far_levels


def vmem_specs(count):
    return [pl.BlockSpec(memory_space=pltpu.VMEM) for _ in range(count)]


def smem_specs(count):
    return [pl.BlockSpec(memory_space=pltpu.SMEM) for _ in range(count)]


def on_device(queries, keys, values, out_grad, block_list, causal):
    tok_rows, feat = queries.shape
    blocks_here = tok_rows // BLOCK
    entries = block_list.shape[1]
    head_size = feat // HEADS
    scale = head_size ** (-0.5)
    stat_cols = HEADS + HEADS * entries

    kv_own = jnp.concatenate([keys, values], 1)
    qg_own = jnp.concatenate([queries, out_grad], 1)
    kv_near = from_behind(kv_own, "ctx", 1)
    qg_next = from_behind(qg_own, "ctx", -1)
    q_kernel, far_levels = query_side(blocks_here, entries, head_size, scale)
    distances = [2 ** (level - 1) // blocks_here for level in far_levels]
    kv_far = [from_behind(kv_own, "ctx", distance) for distance in distances]

    s_kernel, _ = query_side(blocks_here, entries, head_size, scale, with_grads=False)
    stats = pl.pallas_call(
        s_kernel,
        out_shape=jax.ShapeDtypeStruct((stat_cols, tok_rows), jnp.float32),
        in_specs=smem_specs(2) + vmem_specs(4 + len(kv_far)),
        out_specs=vmem_specs(1)[0],
    )(block_list, causal, queries, out_grad, kv_own, kv_near, *kv_far)
    stats_next = from_behind(stats, "ctx", -1)

    query_grad, *terms = pl.pallas_call(
        q_kernel,
        out_shape=(jax.ShapeDtypeStruct((tok_rows, feat), jnp.bfloat16),)
        + tuple(jax.ShapeDtypeStruct((tok_rows, 2 * feat), jnp.bfloat16) for _ in far_levels),
        in_specs=smem_specs(2) + vmem_specs(4 + len(kv_far)),
        out_specs=tuple(vmem_specs(1 + len(far_levels))),
    )(block_list, causal, queries, out_grad, kv_own, kv_near, *kv_far)

    terms_back = [from_behind(term, "ctx", -distance) for term, distance in zip(terms, distances)]

    k_kernel, _ = key_side(blocks_here, entries, head_size, scale)
    key_grad, value_grad = pl.pallas_call(
        k_kernel,
        out_shape=(
            jax.ShapeDtypeStruct((tok_rows, feat), jnp.bfloat16),
            jax.ShapeDtypeStruct((tok_rows, feat), jnp.bfloat16),
        ),
        in_specs=smem_specs(2) + vmem_specs(5 + len(terms_back)),
        out_specs=tuple(vmem_specs(2)),
    )(block_list, causal, kv_own, qg_own, qg_next, stats, stats_next, *terms_back)
    return (query_grad, key_grad, value_grad)


def solution(mesh):
    return jax.shard_map(
        on_device,
        mesh=mesh,
        in_specs=(
            P(("dp", "ctx"), None),
            P(("dp", "ctx"), None),
            P(("dp", "ctx"), None),
            P(("dp", "ctx"), None),
            P(("dp", "ctx"), None),
            P(("dp", "ctx")),
        ),
        out_specs=(P(("dp", "ctx"), None), P(("dp", "ctx"), None), P(("dp", "ctx"), None)),
        check_vma=False,
    )
```

```python
import jax
import jax.numpy as jnp
from jax import lax
from jax.experimental import pallas as pl
from jax.experimental.pallas import tpu as pltpu
from jax.sharding import PartitionSpec as P

BLOCK = 128
HEADS = 2


def from_behind(value, axis, steps):
    count = lax.axis_size(axis)
    initial, last = (max(0, -steps), min(count, count - steps))
    return lax.ppermute(value, axis, [(source, source + steps) for source in range(initial, last)])


def dot_nt(a, b):
    return lax.dot_general(a, b, (((1,), (1,)), ((), ())), preferred_element_type=jnp.float32)


def dot_tn(a, b):
    return lax.dot_general(a, b, (((0,), (0,)), ((), ())), preferred_element_type=jnp.float32)


def dot_nn(a, b):
    return lax.dot_general(a, b, (((1,), (0,)), ((), ())), preferred_element_type=jnp.float32)


def upper_mask():
    rows = lax.broadcasted_iota(jnp.int32, (BLOCK, BLOCK), 0)
    cols = lax.broadcasted_iota(jnp.int32, (BLOCK, BLOCK), 1)
    return rows <= cols


def make_levels(blocks_here, entries):
    kinds = []
    for level in range(entries):
        reach = 2 ** (level - 1) if level > 0 else 0
        kinds.append((level, reach, "own" if level == 0 else ("near" if reach <= blocks_here else "far")))
    return kinds


def query_side(blocks_here, entries, head_size, scale):
    kinds = make_levels(blocks_here, entries)
    far_levels = [level for level, _, kind in kinds if kind == "far"]

    def kernel(list_ref, causal_ref, q_ref, g_ref, own_ref, near_ref, *rest):
        count = len(far_levels)
        far_refs = dict(zip(far_levels, rest[:count]))
        dq_ref, stats_ref = rest[count : count + 2]
        term_refs = dict(zip(far_levels, rest[count + 2 :]))
        upper = upper_mask()
        for block in range(blocks_here):
            rows = slice(block * BLOCK, (block + 1) * BLOCK)
            valid = [list_ref[block, level] >= 0 for level in range(entries)]
            self_ok = jnp.logical_or(upper, causal_ref[block] == 0)
            for head in range(HEADS):
                kcols = slice(head * head_size, (head + 1) * head_size)
                vcols = slice((HEADS + head) * head_size, (HEADS + head + 1) * head_size)
                q = q_ref[rows, kcols]
                g = g_ref[rows, kcols]
                keys_at = []
                values_at = []
                for level, reach, kind in kinds:
                    if kind == "own":
                        src, at = own_ref, block
                    elif kind == "near":
                        joined = blocks_here + block - reach
                        src, at = (own_ref, joined - blocks_here) if joined >= blocks_here else (near_ref, joined)
                    else:
                        src, at = far_refs[level], block
                    half = blocks_here * BLOCK
                    keys_at.append(src[at * BLOCK : (at + 1) * BLOCK, kcols])
                    values_at.append(src[half + at * BLOCK : half + (at + 1) * BLOCK, kcols])
                scores = []
                for level in range(entries):
                    s = dot_nt(keys_at[level], q) * scale
                    keep = jnp.logical_and(self_ok, valid[0]) if level == 0 else valid[level]
                    scores.append(jnp.where(keep, s, -jnp.inf))
                top = scores[0].max(axis=0, keepdims=True)
                for level in range(1, entries):
                    top = jnp.maximum(top, scores[level].max(axis=0, keepdims=True))
                total = jnp.zeros_like(top)
                shifted = []
                for level in range(entries):
                    shifted.append(jnp.exp(scores[level] - top))
                    total = total + jnp.sum(shifted[level], axis=0, keepdims=True)
                lse = top + jnp.log(total)
                inverse = 1.0 / total
                probs = []
                dprobs = []
                delta = jnp.zeros_like(top)
                for level in range(entries):
                    p = shifted[level] * inverse
                    dp = dot_nt(values_at[level], g)
                    w = p.astype(jnp.bfloat16).astype(jnp.float32)
                    delta = delta + jnp.sum(w * dp, axis=0, keepdims=True)
                    probs.append(p)
                    dprobs.append(dp)
                dq = jnp.zeros((BLOCK, head_size), jnp.float32)
                for level in range(entries):
                    ds = (probs[level] * (dprobs[level] - delta)).astype(jnp.bfloat16)
                    dq = dq + dot_tn(ds, keys_at[level])
                    if level in term_refs:
                        term_ref = term_refs[level]
                        term_ref[rows, kcols] = (dot_nn(ds, q) * scale).astype(term_ref.dtype)
                        w = probs[level].astype(jnp.bfloat16)
                        term_ref[rows, vcols] = dot_nn(w, g).astype(term_ref.dtype)
                dq_ref[rows, kcols] = (dq * scale).astype(dq_ref.dtype)
                stats_ref[head : head + 1, rows] = delta
                for level in range(entries):
                    row = HEADS + HEADS * level + head
                    stats_ref[row : row + 1, rows] = jnp.where(valid[level], lse, jnp.inf)

    return kernel, far_levels


def key_side(blocks_here, entries, head_size, scale):
    kinds = make_levels(blocks_here, entries)
    far_levels = [level for level, _, kind in kinds if kind == "far"]

    def kernel(list_ref, causal_ref, kv_ref, qg_ref, qg_next_ref, stats_ref, stats_next_ref, *rest):
        count = len(far_levels)
        back_refs = rest[:count]
        dk_ref, dv_ref = rest[count:]
        upper = upper_mask()
        for block in range(blocks_here):
            rows = slice(block * BLOCK, (block + 1) * BLOCK)
            self_ok = jnp.logical_or(upper, causal_ref[block] == 0)
            for head in range(HEADS):
                kcols = slice(head * head_size, (head + 1) * head_size)
                vcols = slice((HEADS + head) * head_size, (HEADS + head + 1) * head_size)
                half = blocks_here * BLOCK
                k = kv_ref[rows, kcols]
                v = kv_ref[half + block * BLOCK : half + (block + 1) * BLOCK, kcols]
                dk = jnp.zeros((BLOCK, head_size), jnp.float32)
                dv = jnp.zeros((BLOCK, head_size), jnp.float32)
                back_k = jnp.zeros((BLOCK, head_size), jnp.float32)
                for back_ref in back_refs:
                    back_k = back_k + back_ref[rows, kcols].astype(jnp.float32)
                    dv = dv + back_ref[rows, vcols].astype(jnp.float32)
                q_tiles, g_tiles, lse_rows, delta_rows = [], [], [], []
                for level, reach, kind in kinds:
                    if kind == "far":
                        continue
                    if kind == "own":
                        src, st, at = qg_ref, stats_ref, block
                    elif kind == "near":
                        joined = block + reach
                        if joined < blocks_here:
                            src, st, at = qg_ref, stats_ref, joined
                        else:
                            src, st, at = qg_next_ref, stats_next_ref, joined - blocks_here
                    qrows = slice(at * BLOCK, (at + 1) * BLOCK)
                    row = HEADS + HEADS * level + head
                    q_tiles.append(src[qrows, kcols])
                    g_tiles.append(src[half + at * BLOCK : half + (at + 1) * BLOCK, kcols])
                    lse_rows.append(st[row : row + 1, qrows])
                    delta_rows.append(st[head : head + 1, qrows])
                q_cat = jnp.concatenate(q_tiles, axis=0)
                g_cat = jnp.concatenate(g_tiles, axis=0)
                lse = jnp.concatenate(lse_rows, axis=1)
                delta = jnp.concatenate(delta_rows, axis=1)
                bias = [jnp.where(self_ok, 0.0, -jnp.inf), jnp.zeros((BLOCK, BLOCK * (len(q_tiles) - 1)), jnp.float32)]
                s = dot_nt(k, q_cat) * scale + jnp.concatenate(bias, axis=1)
                p = jnp.exp(s - lse)
                w = p.astype(jnp.bfloat16)
                dp = dot_nt(v, g_cat)
                ds = (p * (dp - delta)).astype(jnp.bfloat16)
                dk = dk + dot_nn(ds, q_cat)
                dv = dv + dot_nn(w, g_cat)
                dk_ref[rows, kcols] = (dk * scale + back_k).astype(dk_ref.dtype)
                dv_ref[rows, kcols] = dv.astype(dv_ref.dtype)

    return kernel, far_levels


def vmem_specs(count):
    return [pl.BlockSpec(memory_space=pltpu.VMEM) for _ in range(count)]


def smem_specs(count):
    return [pl.BlockSpec(memory_space=pltpu.SMEM) for _ in range(count)]


def on_device(queries, keys, values, out_grad, block_list, causal):
    tok_rows, feat = queries.shape
    blocks_here = tok_rows // BLOCK
    entries = block_list.shape[1]
    head_size = feat // HEADS
    scale = head_size ** (-0.5)
    stat_cols = HEADS + HEADS * entries

    kv_own = jnp.concatenate([keys, values], 0)
    qg_own = jnp.concatenate([queries, out_grad], 0)
    kv_near = from_behind(kv_own, "ctx", 1)
    qg_next = from_behind(qg_own, "ctx", -1)
    q_kernel, far_levels = query_side(blocks_here, entries, head_size, scale)
    distances = [2 ** (level - 1) // blocks_here for level in far_levels]
    kv_far = [from_behind(kv_own, "ctx", distance) for distance in distances]

    query_grad, stats, *terms = pl.pallas_call(
        q_kernel,
        out_shape=(
            jax.ShapeDtypeStruct((tok_rows, feat), jnp.bfloat16),
            jax.ShapeDtypeStruct((stat_cols, tok_rows), jnp.float32),
        )
        + tuple(jax.ShapeDtypeStruct((tok_rows, 2 * feat), jnp.bfloat16) for _ in far_levels),
        in_specs=smem_specs(2) + vmem_specs(4 + len(kv_far)),
        out_specs=tuple(vmem_specs(2 + len(far_levels))),
    )(block_list, causal, queries, out_grad, kv_own, kv_near, *kv_far)

    stats_next = from_behind(stats, "ctx", -1)
    terms_back = [from_behind(term, "ctx", -distance) for term, distance in zip(terms, distances)]

    k_kernel, _ = key_side(blocks_here, entries, head_size, scale)
    key_grad, value_grad = pl.pallas_call(
        k_kernel,
        out_shape=(
            jax.ShapeDtypeStruct((tok_rows, feat), jnp.bfloat16),
            jax.ShapeDtypeStruct((tok_rows, feat), jnp.bfloat16),
        ),
        in_specs=smem_specs(2) + vmem_specs(5 + len(terms_back)),
        out_specs=tuple(vmem_specs(2)),
    )(block_list, causal, kv_own, qg_own, qg_next, stats, stats_next, *terms_back)
    return (query_grad, key_grad, value_grad)


def solution(mesh):
    return jax.shard_map(
        on_device,
        mesh=mesh,
        in_specs=(
            P(("dp", "ctx"), None),
            P(("dp", "ctx"), None),
            P(("dp", "ctx"), None),
            P(("dp", "ctx"), None),
            P(("dp", "ctx"), None),
            P(("dp", "ctx")),
        ),
        out_specs=(P(("dp", "ctx"), None), P(("dp", "ctx"), None), P(("dp", "ctx"), None)),
        check_vma=False,
    )
```
